32 devices in a mesh: mem: 8 (over y, x, core), tile: 4 (over z).
Axes of the slice: x: 2, y: 2, z: 4, core: 2. Of those that a mesh axis runs over, the one named last changes fastest.
Arguments:
- perturb: bfloat16 [40, 2, 2, 256, 512], P('mem', None, None, None, 'tile'), may hold values from -6 to 6
- coef_x: float32 [2, 256, 512], P(None, None, 'tile'), may hold values from 0.25 to 0.5
- coef_y: float32 [2, 256, 512], P(None, None, 'tile'), may hold values from 0.25 to 0.5
- obs_values: float32 [65536], P(('mem', 'tile')), may hold values from -12 to 12
- obs_tile: int32 [65536, 1], P(('mem', 'tile')), may hold values from 0 to 3; in each aligned block of 2048 rows (0 to 2047, 2048 to 4095, ...) at most 1536 rows name the same one
- obs_cell: int32 [65536], P(('mem', 'tile')), may hold values from 0 to 131071
Outputs:
- increment: float32 [256, 2, 2, 512], P('mem', None, None, 'tile')
The draws below stay inside these ranges and needn't reach their ends.
Inputs may be any that keep to these rules, and one draw needn't show every extreme that they name: `obs_tile`: among the 2048 observations of one device no tile is named more than 1536 times, and in every draw some device names some tile exactly 1536 times.
All inputs are finite; a program needn't handle non-finite values.
Results may differ from the reference program's by a relative error of at most 0.0003.
Values sent between devices are 32-bit elements; how exact they have to be, the bound alone decides.
No kernel may reach another device: no remote copies, remote signals or barrier semaphores. Data moves between devices by JAX's collectives and lax.ppermute only.
A program may use at most 64 MiB of HBM per device.

```python
import math
import jax
import jax.numpy as jnp
import numpy as np
from jax import lax

FIELDS = 2
LEVELS = 2
SWEEPS = 6
LAT = 256
LON_DEV = 128
OBS_DEV = 2048
MEMBERS = 40
TILES = 4
NLON = 512
OBS_TOTAL = 65536
CAP = 1536


def plant(values, key, low, largest):
    longest = values.shape.index(max(values.shape))
    spots = []
    for shift in (0, 1):
        where = [jax.random.randint(jax.random.fold_in(key, axis), (), 0, length) for axis, length in enumerate(values.shape)]
        where[longest] = (where[longest] + shift) % values.shape[longest]
        spots.append(tuple(where))
    return values.at[spots[0]].set(low).at[spots[1]].set(largest)


def with_spikes(values, key, source, target, blocks, factor):
    owner, partner = [(jnp.arange(values.shape[position]) // (values.shape[position] // blocks)).reshape([-1 if axis == position else 1 for axis in range(values.ndim)]) for position in (source, target)]
    chosen = jax.random.permutation(key, blocks)[partner]
    strong = (owner == chosen) | (owner == (partner + blocks // 2) % blocks)
    return jnp.where(strong, factor * values, values)


def block_levels(key, shape, shards, low, largest):
    def one(position, parts):
        heights = jax.random.uniform(jax.random.fold_in(jax.random.fold_in(key, 6), position), (parts,), jnp.float32, low / len(shards), largest / len(shards))
        return jnp.repeat(jnp.exp(heights), shape[position] // parts).reshape((-1,) + (1,) * (len(shape) - position - 1))

    gain = one(*shards[0])
    for cut in shards[1:]:
        gain = gain * one(*cut)
    return gain


def shared_out(rng, own, number, rows, number_of, top, limit, slope):
    order = jax.random.permutation(rng, number_of)
    crowded, usual = shares(number_of, rows * top, limit, slope, True), shares(number_of, rows * top, limit, slope, False)
    places = jnp.arange(number_of)

    def named(lengths, turn):
        used = int((lengths > 0).sum())
        fixed = max(1, used // 4)
        shifted = fixed + (places - fixed + turn * (used - fixed)) % max(1, number_of - fixed)
        return jnp.zeros((number_of,), jnp.int32).at[order[jnp.where(places < fixed, places, shifted)]].set(jnp.asarray(lengths, jnp.int32))

    lengths = jnp.where(number % 4 == 0, named(crowded, number // 4), named(usual, number - number // 4 - 1))
    mixed = jax.random.permutation(jax.random.fold_in(own, 3), number_of)
    source_of, taker = mixed[0:number_of // 2 * 2:2], mixed[1:number_of // 2 * 2:2]
    slack = jnp.minimum(lengths[source_of] - 1, limit - lengths[taker]) // 2
    slack = jnp.where((source_of == order[0]) | (taker == order[0]) | (lengths[taker] == 0), 0, jnp.maximum(slack, 0))
    shifted = jax.random.randint(jax.random.fold_in(own, 4), (number_of // 2,), 0, 1 << 20) % (slack + 1)
    lengths = lengths.at[source_of].add(-shifted).at[taker].add(shifted)
    items = jnp.searchsorted(jnp.cumsum(lengths), jnp.arange(rows * top), side="right").astype(jnp.int32)
    listing = items.reshape(top, rows).T
    listing = listing[jax.random.permutation(jax.random.fold_in(own, 1), rows)]
    turn = jax.random.randint(jax.random.fold_in(own, 2), (rows, 1), 0, top)
    return jnp.take_along_axis(listing, (jnp.arange(top)[None, :] + turn) % top, axis=1)


def shares(count, total, most, skew, full):
    loads = [(1 << 20) // math.isqrt(grade ** skew) + 1 for grade in range(1, count + 1)]
    largest = most if full else min(most, max(-(-total // count), total * loads[0] // sum(loads)))
    least = 1 if total - largest >= count - 1 else 0
    counts, spare = [largest] + [least] * (count - 1), total - largest - least * (count - 1)
    while spare > 0:
        movable = [i for i in range(1, count) if counts[i] < largest] or [i for i in range(1, count) if counts[i] < most]
        pool, budget = sum([loads[i] for i in movable]), spare
        for i in movable:
            extra = min(most - counts[i], max(1, budget * loads[i] // pool), spare)
            counts[i] = counts[i] + extra
            spare = spare - extra
    return np.array(counts)


def gaussian(rng, shape, scale, reach, cuts=(), held_as=jnp.bfloat16):
    gain = block_levels(rng, shape, cuts, -0.22, 0.18) if cuts else 1.0
    array = jax.random.normal(rng, shape, jnp.float32) * scale * gain
    return jnp.minimum(jnp.maximum(array, -reach), reach).astype(held_as)


def noise_with(own_key, shape, spread, most, cuts, heavy, kind=jnp.bfloat16):
    drawn = spread * jax.random.normal(own_key, shape, jnp.float32)
    if cuts:
        drawn = drawn * block_levels(own_key, shape, cuts, -0.22, 0.18)
    return jnp.clip(with_spikes(drawn, jax.random.fold_in(own_key, 3), *heavy), -most, most).astype(kind)


def setup_inputs(seed: int = 0) -> dict:
    streams_of = jax.random.split(jax.random.key(seed), 7)
    perturb = noise_with(streams_of[0], (MEMBERS, FIELDS, LEVELS, LAT, NLON), 1.0, 6.0, ((0, 8), (4, 4)), (0, 3, 8, 2.0))
    coef_x = jnp.clip(0.25 + 0.25 * jax.random.uniform(streams_of[1], (LEVELS, LAT, NLON), jnp.float32) ** block_levels(streams_of[1], (LEVELS, LAT, NLON), ((2, 4),), -0.2, 0.2), 0.25, 0.5)
    coef_y = jnp.clip(0.25 + 0.25 * jax.random.uniform(streams_of[2], (LEVELS, LAT, NLON), jnp.float32) ** block_levels(streams_of[2], (LEVELS, LAT, NLON), ((2, 4),), -0.2, 0.2), 0.25, 0.5)
    obs_values = gaussian(streams_of[3], (OBS_TOTAL,), 3.0, 12.0, ((0, 32),), jnp.float32)
    obs_tile_keys = jax.random.split(jax.random.fold_in(streams_of[4], 1), OBS_TOTAL // OBS_DEV)
    obs_tile_turns = jax.random.permutation(jax.random.fold_in(streams_of[4], 3), OBS_TOTAL // OBS_DEV)
    obs_tile = jax.vmap(lambda own, number: shared_out(jax.random.fold_in(streams_of[4], 2), own, number, OBS_DEV, TILES, 1, CAP, 2))(obs_tile_keys, obs_tile_turns).reshape((OBS_TOTAL, 1))
    obs_cell = plant(jax.random.randint(streams_of[5], (OBS_TOTAL,), 0, FIELDS * LEVELS * LAT * LON_DEV), jax.random.fold_in(streams_of[5], 1), 0, (FIELDS * LEVELS * LAT * LON_DEV) - 1).astype(jnp.int32)
    return {"perturb": perturb, "coef_x": coef_x, "coef_y": coef_y, "obs_values": obs_values, "obs_tile": obs_tile, "obs_cell": obs_cell}


def sweep_east(field, coef):
    flux = coef * (jnp.roll(field, -1, axis=-1) - field)
    return field + flux - jnp.roll(flux, 1, axis=-1)


def sweep_north(field, coef):
    flux = coef[..., :-1, :] * (field[..., 1:, :] - field[..., :-1, :])
    zero_row = jnp.zeros(field.shape[:-2] + (1, field.shape[-1]), jnp.float32)
    upper = jnp.concatenate([flux, zero_row], axis=-2)
    lower = jnp.concatenate([zero_row, flux], axis=-2)
    return field + upper - lower


def reference(perturb, coef_x, coef_y, obs_values, obs_tile, obs_cell):
    span = LAT * LON_DEV
    channel = obs_cell // span
    remain = obs_cell % span
    row = remain // LON_DEV
    column = obs_tile[:, 0] * LON_DEV + remain % LON_DEV
    flat = channel * (LAT * NLON) + row * NLON + column
    adjoint_field = jnp.zeros((FIELDS * LEVELS * LAT * NLON,), jnp.float32).at[flat].add(obs_values)
    adjoint_field = adjoint_field.reshape(FIELDS, LEVELS, LAT, NLON)

    def accumulate(total, member):
        widened = member.astype(jnp.float32)
        product = jnp.sum(widened * adjoint_field, axis=0)
        for step in range(SWEEPS):
            product = sweep_east(product, coef_x)
        for step in range(SWEEPS):
            product = sweep_north(product, coef_y)
        return total + widened * product[None], None

    start = jnp.zeros((FIELDS, LEVELS, LAT, NLON), jnp.float32)
    total, unused = lax.scan(accumulate, start, perturb)
    result = total / (MEMBERS - 1)
    return jnp.transpose(result, (2, 0, 1, 3))
```

```python
import jax
import jax.numpy as jnp
from jax import lax
from jax.sharding import PartitionSpec as P

FIELDS = 2
LEVELS = 2
SWEEPS = 6
LAT = 256


def sweep_north(field, coef):
    flux = coef[..., :-1, :] * (field[..., 1:, :] - field[..., :-1, :])
    zero_row = jnp.zeros(field.shape[:-2] + (1, field.shape[-1]), jnp.float32)
    upper = jnp.concatenate([flux, zero_row], axis=-2)
    lower = jnp.concatenate([zero_row, flux], axis=-2)
    return field + upper - lower


def deposit(values, cells, rows, cols, width):
    index = cells.astype(jnp.int32)
    span = rows * cols
    channel = index // span
    remain = index % span
    row = remain // cols
    column = channel * cols + remain % cols
    row_hit = (row[:, None] == jnp.arange(rows, dtype=jnp.int32)[None, :]).astype(jnp.bfloat16)
    hit = column[:, None] == jnp.arange(width, dtype=jnp.int32)[None, :]
    rounded = lax.reduce_precision(values, exponent_bits=8, mantissa_bits=7)
    high = rounded.astype(jnp.bfloat16)
    low = (values - rounded).astype(jnp.bfloat16)
    zero = jnp.zeros((), jnp.bfloat16)
    weighted = jnp.concatenate(
        [jnp.where(hit, high[:, None], zero), jnp.where(hit, low[:, None], zero)], axis=1
    )
    both = jnp.einsum("nr,nj->rj", row_hit, weighted, preferred_element_type=jnp.float32)
    return both[:, :width] + both[:, width:]


def allreduce_mem(x, mems):
    bits = mems.bit_length() - 1
    assert 1 << bits == mems
    me = lax.axis_index("mem")
    for b in range(bits):
        pairs = [(i, i ^ (1 << b)) for i in range(mems)]
        mine = (me >> b) & 1
        halves = x.reshape((2, x.shape[0] // 2) + x.shape[1:])
        keep = lax.dynamic_index_in_dim(halves, mine, 0, keepdims=False)
        send = lax.dynamic_index_in_dim(halves, 1 - mine, 0, keepdims=False)
        x = keep + lax.ppermute(send, "mem", pairs)
    for b in reversed(range(bits)):
        pairs = [(i, i ^ (1 << b)) for i in range(mems)]
        mine = (me >> b) & 1
        other = lax.ppermute(x, "mem", pairs)
        out = jnp.zeros((2,) + x.shape, x.dtype)
        out = lax.dynamic_update_index_in_dim(out, x, mine, 0)
        out = lax.dynamic_update_index_in_dim(out, other, 1 - mine, 0)
        x = out.reshape((-1,) + x.shape[1:])
    return x


def on_device(perturb, coef_x, coef_y, obs_values, obs_tile, obs_cell):
    tiles = lax.axis_size("tile")
    mems = lax.axis_size("mem")
    kl, nf, nl, nr, nq = perturb.shape
    members = kl * mems
    width = nf * nl * nq
    halo = SWEEPS

    forward = [(i, (i + 1) % tiles) for i in range(tiles)]
    backward = [((i + 1) % tiles, i) for i in range(tiles)]
    coef_left = lax.ppermute(coef_x[..., -halo:], "tile", forward)
    coef_right = lax.ppermute(coef_x[..., :halo], "tile", backward)

    target = obs_tile[:, 0]
    dest = jnp.arange(tiles, dtype=jnp.int32)[:, None]
    values = jnp.where(target[None, :] == dest, obs_values[None, :], 0.0)
    cells = jnp.broadcast_to(obs_cell.astype(jnp.float32)[None, :], values.shape)
    outgoing = jnp.stack([values, cells], axis=1)
    incoming = lax.all_to_all(outgoing, "tile", 0, 0, tiled=True)
    field = deposit(incoming[0, 0], incoming[0, 1], nr, nq, width)
    for source in range(1, tiles):
        field = field + deposit(incoming[source, 0], incoming[source, 1], nr, nq, width)
    field = allreduce_mem(field, mems)
    adjoint = jnp.transpose(field.reshape(nr, nf, nl, nq), (1, 2, 0, 3))

    widened = perturb.astype(jnp.float32)
    product = jnp.sum(widened * adjoint[None], axis=1)
    left = lax.ppermute(product[..., -halo:], "tile", forward)
    right = lax.ppermute(product[..., :halo], "tile", backward)
    value = jnp.concatenate([left, product, right], axis=-1)
    coef = jnp.concatenate([coef_left, coef_x, coef_right], axis=-1)
    for step in range(SWEEPS):
        flux = coef[..., :-1] * (value[..., 1:] - value[..., :-1])
        value = value[..., 1:-1] + flux[..., 1:] - flux[..., :-1]
        coef = coef[..., 1:-1]
    product = value
    for step in range(SWEEPS):
        product = sweep_north(product, coef_y)
    part = jnp.einsum("kflyx,klyx->yflx", widened, product)
    blocks = part.reshape((mems, nr // mems) + part.shape[1:])
    summed = lax.all_to_all(blocks, "mem", 0, 0, tiled=True).sum(axis=0)
    return summed / (members - 1)


def solution(mesh):
    return jax.shard_map(
        on_device,
        mesh=mesh,
        in_specs=(
            P("mem", None, None, None, "tile"),
            P(None, None, "tile"),
            P(None, None, "tile"),
            P(("mem", "tile")),
            P(("mem", "tile"), None),
            P(("mem", "tile")),
        ),
        out_specs=P("mem", None, None, "tile"),
        check_vma=False,
    )
```

```python
import jax
import jax.numpy as jnp
from jax import lax
from jax.sharding import PartitionSpec as P

FIELDS = 2
LEVELS = 2
SWEEPS = 6
LAT = 256


def sweep_north(field, coef):
    flux = coef[..., :-1, :] * (field[..., 1:, :] - field[..., :-1, :])
    zero_row = jnp.zeros(field.shape[:-2] + (1, field.shape[-1]), jnp.float32)
    upper = jnp.concatenate([flux, zero_row], axis=-2)
    lower = jnp.concatenate([zero_row, flux], axis=-2)
    return field + upper - lower


def deposit(values, cells, rows, cols, width):
    index = cells.astype(jnp.int32)
    span = rows * cols
    channel = index // span
    remain = index % span
    row = remain // cols
    column = channel * cols + remain % cols
    row_hit = (row[:, None] == jnp.arange(rows, dtype=jnp.int32)[None, :]).astype(jnp.bfloat16)
    hit = column[:, None] == jnp.arange(width, dtype=jnp.int32)[None, :]
    rounded = lax.reduce_precision(values, exponent_bits=8, mantissa_bits=7)
    high = rounded.astype(jnp.bfloat16)
    low = (values - rounded).astype(jnp.bfloat16)
    zero = jnp.zeros((), jnp.bfloat16)
    weighted = jnp.concatenate(
        [jnp.where(hit, high[:, None], zero), jnp.where(hit, low[:, None], zero)], axis=1
    )
    both = jnp.einsum("nr,nj->rj", row_hit, weighted, preferred_element_type=jnp.float32)
    return both[:, :width] + both[:, width:]


def exchange(blocks, axis, count):
    me = lax.axis_index(axis)
    out = jnp.zeros_like(blocks)
    out = lax.dynamic_update_index_in_dim(out, lax.dynamic_index_in_dim(blocks, me, 0, keepdims=False), me, 0)
    for s in range(1, count):
        pairs = [(i, i ^ s) for i in range(count)]
        sent = lax.dynamic_index_in_dim(blocks, me ^ s, 0, keepdims=False)
        got = lax.ppermute(sent, axis, pairs)
        out = lax.dynamic_update_index_in_dim(out, got, me ^ s, 0)
    return out


def scatter_sum(x, axis, count):
    blocks = x.reshape((count, x.shape[0] // count) + x.shape[1:])
    return exchange(blocks, axis, count).sum(axis=0)


def gather_blocks(x, axis, count):
    me = lax.axis_index(axis)
    out = jnp.zeros((count,) + x.shape, x.dtype)
    out = lax.dynamic_update_index_in_dim(out, x, me, 0)
    for s in range(1, count):
        pairs = [(i, i ^ s) for i in range(count)]
        out = lax.dynamic_update_index_in_dim(out, lax.ppermute(x, axis, pairs), me ^ s, 0)
    return out.reshape((-1,) + x.shape[1:])


def on_device(perturb, coef_x, coef_y, obs_values, obs_tile, obs_cell):
    tiles = lax.axis_size("tile")
    mems = lax.axis_size("mem")
    kl, nf, nl, nr, nq = perturb.shape
    members = kl * mems
    width = nf * nl * nq
    halo = SWEEPS

    assert tiles & (tiles - 1) == 0 and mems & (mems - 1) == 0
    forward = [(i, (i + 1) % tiles) for i in range(tiles)]
    backward = [((i + 1) % tiles, i) for i in range(tiles)]

    target = obs_tile[:, 0]
    dest = jnp.arange(tiles, dtype=jnp.int32)[:, None]
    values = jnp.where(target[None, :] == dest, obs_values[None, :], 0.0)
    cells = jnp.broadcast_to(obs_cell.astype(jnp.float32)[None, :], values.shape)
    incoming = exchange(jnp.stack([values, cells], axis=1), "tile", tiles)
    field = deposit(incoming[0, 0], incoming[0, 1], nr, nq, width)
    for source in range(1, tiles):
        field = field + deposit(incoming[source, 0], incoming[source, 1], nr, nq, width)
    field = gather_blocks(scatter_sum(field, "mem", mems), "mem", mems)
    adjoint = jnp.transpose(field.reshape(nr, nf, nl, nq), (1, 2, 0, 3))

    widened = perturb.astype(jnp.float32)
    product = jnp.sum(widened * adjoint[None], axis=1)
    joined = jnp.concatenate([product, coef_x[None]], axis=0)
    left = lax.ppermute(joined[..., -halo:], "tile", forward)
    right = lax.ppermute(joined[..., :halo], "tile", backward)
    joined = jnp.concatenate([left, joined, right], axis=-1)
    value, coef = joined[:-1], joined[-1]
    for step in range(SWEEPS):
        flux = coef[..., :-1] * (value[..., 1:] - value[..., :-1])
        value = value[..., 1:-1] + flux[..., 1:] - flux[..., :-1]
        coef = coef[..., 1:-1]
    product = value
    for step in range(SWEEPS):
        product = sweep_north(product, coef_y)
    part = jnp.einsum("kflyx,klyx->yflx", widened, product)
    summed = scatter_sum(part, "mem", mems)
    return summed / (members - 1)


def solution(mesh):
    return jax.shard_map(
        on_device,
        mesh=mesh,
        in_specs=(
            P("mem", None, None, None, "tile"),
            P(None, None, "tile"),
            P(None, None, "tile"),
            P(("mem", "tile")),
            P(("mem", "tile"), None),
            P(("mem", "tile")),
        ),
        out_specs=P("mem", None, None, "tile"),
        check_vma=False,
    )
```

```python
import jax
import jax.numpy as jnp
from jax import lax
from jax.sharding import PartitionSpec as P

FIELDS = 2
LEVELS = 2
SWEEPS = 6
LAT = 256


def sweep_north(field, coef):
    flux = coef[..., :-1, :] * (field[..., 1:, :] - field[..., :-1, :])
    zero_row = jnp.zeros(field.shape[:-2] + (1, field.shape[-1]), jnp.float32)
    upper = jnp.concatenate([flux, zero_row], axis=-2)
    lower = jnp.concatenate([zero_row, flux], axis=-2)
    return field + upper - lower


def deposit(values, cells, rows, ext, width):
    index = cells.astype(jnp.int32)
    line = index // ext
    channel = line // rows
    row = line % rows
    column = channel * ext + index % ext
    row_hit = (row[:, None] == jnp.arange(rows, dtype=jnp.int32)[None, :]).astype(jnp.bfloat16)
    hit = column[:, None] == jnp.arange(width, dtype=jnp.int32)[None, :]
    rounded = lax.reduce_precision(values, exponent_bits=8, mantissa_bits=7)
    high = rounded.astype(jnp.bfloat16)
    low = (values - rounded).astype(jnp.bfloat16)
    zero = jnp.zeros((), jnp.bfloat16)
    weighted = jnp.concatenate(
        [jnp.where(hit, high[:, None], zero), jnp.where(hit, low[:, None], zero)], axis=1
    )
    both = jnp.einsum("nr,nj->rj", row_hit, weighted, preferred_element_type=jnp.float32)
    return both[:, :width] + both[:, width:]


def exchange(blocks, axis, count):
    me = lax.axis_index(axis)
    out = jnp.zeros_like(blocks)
    out = lax.dynamic_update_index_in_dim(out, lax.dynamic_index_in_dim(blocks, me, 0, keepdims=False), me, 0)
    for s in range(1, count):
        pairs = [(i, i ^ s) for i in range(count)]
        sent = lax.dynamic_index_in_dim(blocks, me ^ s, 0, keepdims=False)
        got = lax.ppermute(sent, axis, pairs)
        out = lax.dynamic_update_index_in_dim(out, got, me ^ s, 0)
    return out


def scatter_sum(x, axis, count):
    blocks = x.reshape((count, x.shape[0] // count) + x.shape[1:])
    return exchange(blocks, axis, count).sum(axis=0)


def gather_blocks(x, axis, count):
    me = lax.axis_index(axis)
    out = jnp.zeros((count,) + x.shape, x.dtype)
    out = lax.dynamic_update_index_in_dim(out, x, me, 0)
    for s in range(1, count):
        pairs = [(i, i ^ s) for i in range(count)]
        out = lax.dynamic_update_index_in_dim(out, lax.ppermute(x, axis, pairs), me ^ s, 0)
    return out.reshape((-1,) + x.shape[1:])


def on_device(perturb, coef_x, coef_y, obs_values, obs_tile, obs_cell):
    tiles = lax.axis_size("tile")
    mems = lax.axis_size("mem")
    kl, nf, nl, nr, nq = perturb.shape
    members = kl * mems
    halo = SWEEPS
    ext = nq + 2 * halo
    width = nf * nl * ext

    assert tiles >= 3 and tiles & (tiles - 1) == 0 and mems & (mems - 1) == 0
    forward = [(i, (i + 1) % tiles) for i in range(tiles)]
    backward = [((i + 1) % tiles, i) for i in range(tiles)]
    widened = perturb.astype(jnp.float32)
    edges = jnp.concatenate([widened.reshape((kl * nf * nl, nr, nq)), coef_x], axis=0)
    left = lax.ppermute(edges[..., -halo:], "tile", forward)
    right = lax.ppermute(edges[..., :halo], "tile", backward)
    edges = jnp.concatenate([left, edges, right], axis=-1)
    coef = edges[kl * nf * nl:]
    spread = edges[: kl * nf * nl].reshape((kl, nf, nl, nr, ext))

    target = obs_tile[:, 0]
    channel_row = obs_cell // nq
    column = obs_cell % nq
    dest = jnp.arange(tiles, dtype=jnp.int32)[:, None]
    apart = (target[None, :] - dest) % tiles
    apart = jnp.where(apart > tiles // 2, apart - tiles, apart)
    place = apart * nq + column[None, :] + halo
    inside = (place >= 0) & (place < ext)
    values = jnp.where(inside, obs_values[None, :], 0.0)
    cells = jnp.where(inside, channel_row[None, :] * ext + place, 0).astype(jnp.float32)
    incoming = exchange(jnp.stack([values, cells], axis=1), "tile", tiles)
    field = deposit(incoming[0, 0], incoming[0, 1], nr, ext, width)
    for source in range(1, tiles):
        field = field + deposit(incoming[source, 0], incoming[source, 1], nr, ext, width)
    field = gather_blocks(scatter_sum(field, "mem", mems), "mem", mems)
    adjoint = jnp.transpose(field.reshape(nr, nf, nl, ext), (1, 2, 0, 3))

    value = jnp.sum(spread * adjoint[None], axis=1)
    for step in range(SWEEPS):
        flux = coef[..., :-1] * (value[..., 1:] - value[..., :-1])
        value = value[..., 1:-1] + flux[..., 1:] - flux[..., :-1]
        coef = coef[..., 1:-1]
    product = value
    for step in range(SWEEPS):
        product = sweep_north(product, coef_y)
    part = jnp.einsum("kflyx,klyx->yflx", widened, product)
    summed = scatter_sum(part, "mem", mems)
    return summed / (members - 1)


def solution(mesh):
    return jax.shard_map(
        on_device,
        mesh=mesh,
        in_specs=(
            P("mem", None, None, None, "tile"),
            P(None, None, "tile"),
            P(None, None, "tile"),
            P(("mem", "tile")),
            P(("mem", "tile"), None),
            P(("mem", "tile")),
        ),
        out_specs=P("mem", None, None, "tile"),
        check_vma=False,
    )
```

```python
import jax
import jax.numpy as jnp
from jax import lax
from jax.experimental import pallas as pl
from jax.experimental.pallas import tpu as pltpu
from jax.sharding import PartitionSpec as P

FIELDS = 2
LEVELS = 2
SWEEPS = 6
LAT = 256


def sweep_north(field, coef):
    flux = coef[..., :-1, :] * (field[..., 1:, :] - field[..., :-1, :])
    zero_row = jnp.zeros(field.shape[:-2] + (1, field.shape[-1]), jnp.float32)
    upper = jnp.concatenate([flux, zero_row], axis=-2)
    lower = jnp.concatenate([zero_row, flux], axis=-2)
    return field + upper - lower


def deposit(values, cells, rows, cols, width):
    index = cells.astype(jnp.int32)
    span = rows * cols
    channel = index // span
    remain = index % span
    row = remain // cols
    column = channel * cols + remain % cols
    row_hit = (row[:, None] == jnp.arange(rows, dtype=jnp.int32)[None, :]).astype(jnp.bfloat16)
    hit = column[:, None] == jnp.arange(width, dtype=jnp.int32)[None, :]
    rounded = lax.reduce_precision(values, exponent_bits=8, mantissa_bits=7)
    high = rounded.astype(jnp.bfloat16)
    low = (values - rounded).astype(jnp.bfloat16)
    zero = jnp.zeros((), jnp.bfloat16)
    weighted = jnp.concatenate(
        [jnp.where(hit, high[:, None], zero), jnp.where(hit, low[:, None], zero)], axis=1
    )
    both = jnp.einsum("nr,nj->rj", row_hit, weighted, preferred_element_type=jnp.float32)
    return both[:, :width] + both[:, width:]


def exchange(blocks, axis, count):
    me = lax.axis_index(axis)
    out = jnp.zeros_like(blocks)
    out = lax.dynamic_update_index_in_dim(out, lax.dynamic_index_in_dim(blocks, me, 0, keepdims=False), me, 0)
    for s in range(1, count):
        pairs = [(i, i ^ s) for i in range(count)]
        sent = lax.dynamic_index_in_dim(blocks, me ^ s, 0, keepdims=False)
        got = lax.ppermute(sent, axis, pairs)
        out = lax.dynamic_update_index_in_dim(out, got, me ^ s, 0)
    return out


def scatter_sum(x, axis, count):
    blocks = x.reshape((count, x.shape[0] // count) + x.shape[1:])
    return exchange(blocks, axis, count).sum(axis=0)


def gather_blocks(x, axis, count):
    me = lax.axis_index(axis)
    out = jnp.zeros((count,) + x.shape, x.dtype)
    out = lax.dynamic_update_index_in_dim(out, x, me, 0)
    for s in range(1, count):
        pairs = [(i, i ^ s) for i in range(count)]
        out = lax.dynamic_update_index_in_dim(out, lax.ppermute(x, axis, pairs), me ^ s, 0)
    return out.reshape((-1,) + x.shape[1:])


def sweep_kernel(pert_ref, adj_ref, halo_ref, cx_ref, cxh_ref, cy_ref, out_ref):
    kl = pert_ref.shape[0]
    nr, nq = adj_ref.shape[2], adj_ref.shape[3]
    coef = jnp.concatenate([cx_ref[0], cxh_ref[0]], axis=1)
    rows = lax.broadcasted_iota(jnp.int32, (nr, nq), 0)
    north = jnp.where(rows < nr - 1, cy_ref[0], 0.0)
    a0 = adj_ref[0, 0]
    a1 = adj_ref[1, 0]
    acc0 = jnp.zeros((nr, nq), jnp.float32)
    acc1 = jnp.zeros((nr, nq), jnp.float32)
    for k in range(kl):
        p0 = pert_ref[k, 0, 0].astype(jnp.float32)
        p1 = pert_ref[k, 1, 0].astype(jnp.float32)
        v = jnp.concatenate([p0 * a0 + p1 * a1, halo_ref[k, 0]], axis=1)
        for step in range(SWEEPS):
            flux = coef * (pltpu.roll(v, 2 * nq - 1, 1) - v)
            v = v + flux - pltpu.roll(flux, 1, 1)
        v = v[:, :nq]
        for step in range(SWEEPS):
            flux = north * (pltpu.roll(v, nr - 1, 0) - v)
            v = v + flux - pltpu.roll(flux, 1, 0)
        acc0 = acc0 + p0 * v
        acc1 = acc1 + p1 * v
    out_ref[0, 0] = acc0
    out_ref[1, 0] = acc1


def sweeps(perturb, adjoint, halo, coef_x, coef_halo, coef_y):
    kl, nf, nl, nr, nq = perturb.shape
    return pl.pallas_call(
        sweep_kernel,
        grid=(nl,),
        in_specs=[
            pl.BlockSpec((kl, nf, 1, nr, nq), lambda l: (0, 0, l, 0, 0)),
            pl.BlockSpec((nf, 1, nr, nq), lambda l: (0, l, 0, 0)),
            pl.BlockSpec((kl, 1, nr, nq), lambda l: (0, l, 0, 0)),
            pl.BlockSpec((1, nr, nq), lambda l: (l, 0, 0)),
            pl.BlockSpec((1, nr, nq), lambda l: (l, 0, 0)),
            pl.BlockSpec((1, nr, nq), lambda l: (l, 0, 0)),
        ],
        out_specs=pl.BlockSpec((nf, 1, nr, nq), lambda l: (0, l, 0, 0)),
        out_shape=jax.ShapeDtypeStruct((nf, nl, nr, nq), jnp.float32),
    )(perturb, adjoint, halo, coef_x, coef_halo, coef_y)


def on_device(perturb, coef_x, coef_y, obs_values, obs_tile, obs_cell):
    tiles = lax.axis_size("tile")
    mems = lax.axis_size("mem")
    kl, nf, nl, nr, nq = perturb.shape
    members = kl * mems
    width = nf * nl * nq
    halo = SWEEPS

    assert tiles & (tiles - 1) == 0 and mems & (mems - 1) == 0
    forward = [(i, (i + 1) % tiles) for i in range(tiles)]
    backward = [((i + 1) % tiles, i) for i in range(tiles)]

    target = obs_tile[:, 0]
    dest = jnp.arange(tiles, dtype=jnp.int32)[:, None]
    values = jnp.where(target[None, :] == dest, obs_values[None, :], 0.0)
    cells = jnp.broadcast_to(obs_cell.astype(jnp.float32)[None, :], values.shape)
    incoming = exchange(jnp.stack([values, cells], axis=1), "tile", tiles)
    field = deposit(incoming[0, 0], incoming[0, 1], nr, nq, width)
    for source in range(1, tiles):
        field = field + deposit(incoming[source, 0], incoming[source, 1], nr, nq, width)
    field = gather_blocks(scatter_sum(field, "mem", mems), "mem", mems)
    adjoint = jnp.transpose(field.reshape(nr, nf, nl, nq), (1, 2, 0, 3))

    widened = perturb.astype(jnp.float32)
    low_edge = jnp.sum(widened[..., :halo] * adjoint[None, ..., :halo], axis=1)
    high_edge = jnp.sum(widened[..., -halo:] * adjoint[None, ..., -halo:], axis=1)
    left = lax.ppermute(
        jnp.concatenate([high_edge, coef_x[None, ..., -halo:]], axis=0), "tile", forward
    )
    right = lax.ppermute(
        jnp.concatenate([low_edge, coef_x[None, ..., :halo]], axis=0), "tile", backward
    )
    gap = jnp.zeros(left.shape[:-1] + (nq - 2 * halo,), jnp.float32)
    ring = jnp.concatenate([right, gap, left], axis=-1)
    part = sweeps(perturb, adjoint, ring[:-1], coef_x, ring[-1], coef_y)
    blocks = part.reshape((nf, nl, mems, nr // mems, nq))
    blocks = jnp.transpose(blocks, (2, 0, 1, 3, 4))
    summed = jnp.transpose(exchange(blocks, "mem", mems).sum(axis=0), (2, 0, 1, 3))
    return summed / (members - 1)


def solution(mesh):
    return jax.shard_map(
        on_device,
        mesh=mesh,
        in_specs=(
            P("mem", None, None, None, "tile"),
            P(None, None, "tile"),
            P(None, None, "tile"),
            P(("mem", "tile")),
            P(("mem", "tile"), None),
            P(("mem", "tile")),
        ),
        out_specs=P("mem", None, None, "tile"),
        check_vma=False,
    )
```

```python
import jax
import jax.numpy as jnp
from jax import lax
from jax.experimental import pallas as pl
from jax.experimental.pallas import tpu as pltpu
from jax.sharding import PartitionSpec as P

FIELDS = 2
LEVELS = 2
SWEEPS = 6
LAT = 256


def sweep_north(field, coef):
    flux = coef[..., :-1, :] * (field[..., 1:, :] - field[..., :-1, :])
    zero_row = jnp.zeros(field.shape[:-2] + (1, field.shape[-1]), jnp.float32)
    upper = jnp.concatenate([flux, zero_row], axis=-2)
    lower = jnp.concatenate([zero_row, flux], axis=-2)
    return field + upper - lower


def deposit(values, cells, rows, cols, width):
    index = cells.astype(jnp.int32)
    span = rows * cols
    channel = index // span
    remain = index % span
    row = remain // cols
    column = channel * cols + remain % cols
    row_hit = (row[:, None] == jnp.arange(rows, dtype=jnp.int32)[None, :]).astype(jnp.bfloat16)
    hit = column[:, None] == jnp.arange(width, dtype=jnp.int32)[None, :]
    rounded = lax.reduce_precision(values, exponent_bits=8, mantissa_bits=7)
    high = rounded.astype(jnp.bfloat16)
    low = (values - rounded).astype(jnp.bfloat16)
    zero = jnp.zeros((), jnp.bfloat16)
    weighted = jnp.concatenate(
        [jnp.where(hit, high[:, None], zero), jnp.where(hit, low[:, None], zero)], axis=1
    )
    both = jnp.einsum("nr,nj->rj", row_hit, weighted, preferred_element_type=jnp.float32)
    return both[:, :width] + both[:, width:]


def exchange(blocks, axis, count):
    me = lax.axis_index(axis)
    out = jnp.zeros_like(blocks)
    out = lax.dynamic_update_index_in_dim(out, lax.dynamic_index_in_dim(blocks, me, 0, keepdims=False), me, 0)
    for s in range(1, count):
        pairs = [(i, i ^ s) for i in range(count)]
        sent = lax.dynamic_index_in_dim(blocks, me ^ s, 0, keepdims=False)
        got = lax.ppermute(sent, axis, pairs)
        out = lax.dynamic_update_index_in_dim(out, got, me ^ s, 0)
    return out


def scatter_sum(x, axis, count):
    blocks = x.reshape((count, x.shape[0] // count) + x.shape[1:])
    return exchange(blocks, axis, count).sum(axis=0)


def gather_blocks(x, axis, count):
    me = lax.axis_index(axis)
    out = jnp.zeros((count,) + x.shape, x.dtype)
    out = lax.dynamic_update_index_in_dim(out, x, me, 0)
    for s in range(1, count):
        pairs = [(i, i ^ s) for i in range(count)]
        out = lax.dynamic_update_index_in_dim(out, lax.ppermute(x, axis, pairs), me ^ s, 0)
    return out.reshape((-1,) + x.shape[1:])


def sweep_kernel(pert_ref, adj_ref, halo_ref, cx_ref, cxh_ref, cy_ref, out_ref, east_ref):
    kl = pert_ref.shape[0]
    nr, nq = adj_ref.shape[2], adj_ref.shape[3]
    chunk = 32
    rows = lax.broadcasted_iota(jnp.int32, (nr, nq), 0)
    north = jnp.where(rows < nr - 1, cy_ref[0], 0.0)
    out_ref[...] = jnp.zeros(out_ref.shape, jnp.float32)
    for k in range(kl):

        def east(c, carry):
            band = pl.ds(pl.multiple_of(c * chunk, chunk), chunk)
            p0 = pert_ref[k, 0, 0, band, :].astype(jnp.float32)
            p1 = pert_ref[k, 1, 0, band, :].astype(jnp.float32)
            core = p0 * adj_ref[0, 0, band, :] + p1 * adj_ref[1, 0, band, :]
            v = jnp.concatenate([core, halo_ref[k, 0, band, :]], axis=1)
            coef = jnp.concatenate([cx_ref[0, band, :], cxh_ref[0, band, :]], axis=1)
            for step in range(SWEEPS):
                flux = coef * (pltpu.roll(v, 2 * nq - 1, 1) - v)
                v = v + flux - pltpu.roll(flux, 1, 1)
            east_ref[band, :] = v[:, :nq]
            return carry

        lax.fori_loop(0, nr // chunk, east, 0, unroll=True)
        v = east_ref[...]
        for step in range(SWEEPS):
            flux = north * (pltpu.roll(v, nr - 1, 0) - v)
            v = v + flux - pltpu.roll(flux, 1, 0)
        out_ref[0, 0] += pert_ref[k, 0, 0].astype(jnp.float32) * v
        out_ref[1, 0] += pert_ref[k, 1, 0].astype(jnp.float32) * v


def sweeps(perturb, adjoint, halo, coef_x, coef_halo, coef_y):
    kl, nf, nl, nr, nq = perturb.shape
    return pl.pallas_call(
        sweep_kernel,
        grid=(nl,),
        in_specs=[
            pl.BlockSpec((kl, nf, 1, nr, nq), lambda l: (0, 0, l, 0, 0)),
            pl.BlockSpec((nf, 1, nr, nq), lambda l: (0, l, 0, 0)),
            pl.BlockSpec((kl, 1, nr, nq), lambda l: (0, l, 0, 0)),
            pl.BlockSpec((1, nr, nq), lambda l: (l, 0, 0)),
            pl.BlockSpec((1, nr, nq), lambda l: (l, 0, 0)),
            pl.BlockSpec((1, nr, nq), lambda l: (l, 0, 0)),
        ],
        out_specs=pl.BlockSpec((nf, 1, nr, nq), lambda l: (0, l, 0, 0)),
        out_shape=jax.ShapeDtypeStruct((nf, nl, nr, nq), jnp.float32),
        scratch_shapes=[pltpu.VMEM((nr, nq), jnp.float32)],
    )(perturb, adjoint, halo, coef_x, coef_halo, coef_y)


def on_device(perturb, coef_x, coef_y, obs_values, obs_tile, obs_cell):
    tiles = lax.axis_size("tile")
    mems = lax.axis_size("mem")
    kl, nf, nl, nr, nq = perturb.shape
    members = kl * mems
    width = nf * nl * nq
    halo = SWEEPS

    assert tiles & (tiles - 1) == 0 and mems & (mems - 1) == 0
    forward = [(i, (i + 1) % tiles) for i in range(tiles)]
    backward = [((i + 1) % tiles, i) for i in range(tiles)]

    target = obs_tile[:, 0]
    dest = jnp.arange(tiles, dtype=jnp.int32)[:, None]
    values = jnp.where(target[None, :] == dest, obs_values[None, :], 0.0)
    cells = jnp.broadcast_to(obs_cell.astype(jnp.float32)[None, :], values.shape)
    incoming = exchange(jnp.stack([values, cells], axis=1), "tile", tiles)
    field = deposit(incoming[0, 0], incoming[0, 1], nr, nq, width)
    for source in range(1, tiles):
        field = field + deposit(incoming[source, 0], incoming[source, 1], nr, nq, width)
    field = gather_blocks(scatter_sum(field, "mem", mems), "mem", mems)
    adjoint = jnp.transpose(field.reshape(nr, nf, nl, nq), (1, 2, 0, 3))

    widened = perturb.astype(jnp.float32)
    low_edge = jnp.sum(widened[..., :halo] * adjoint[None, ..., :halo], axis=1)
    high_edge = jnp.sum(widened[..., -halo:] * adjoint[None, ..., -halo:], axis=1)
    left = lax.ppermute(
        jnp.concatenate([high_edge, coef_x[None, ..., -halo:]], axis=0), "tile", forward
    )
    right = lax.ppermute(
        jnp.concatenate([low_edge, coef_x[None, ..., :halo]], axis=0), "tile", backward
    )
    gap = jnp.zeros(left.shape[:-1] + (nq - 2 * halo,), jnp.float32)
    ring = jnp.concatenate([right, gap, left], axis=-1)
    part = sweeps(perturb, adjoint, ring[:-1], coef_x, ring[-1], coef_y)
    blocks = part.reshape((nf, nl, mems, nr // mems, nq))
    blocks = jnp.transpose(blocks, (2, 0, 1, 3, 4))
    summed = jnp.transpose(exchange(blocks, "mem", mems).sum(axis=0), (2, 0, 1, 3))
    return summed / (members - 1)


def solution(mesh):
    return jax.shard_map(
        on_device,
        mesh=mesh,
        in_specs=(
            P("mem", None, None, None, "tile"),
            P(None, None, "tile"),
            P(None, None, "tile"),
            P(("mem", "tile")),
            P(("mem", "tile"), None),
            P(("mem", "tile")),
        ),
        out_specs=P("mem", None, None, "tile"),
        check_vma=False,
    )
```

```python
import jax
import jax.numpy as jnp
from jax import lax
from jax.experimental import pallas as pl
from jax.experimental.pallas import tpu as pltpu
from jax.sharding import PartitionSpec as P

FIELDS = 2
LEVELS = 2
SWEEPS = 6
LAT = 256


def sweep_north(field, coef):
    flux = coef[..., :-1, :] * (field[..., 1:, :] - field[..., :-1, :])
    zero_row = jnp.zeros(field.shape[:-2] + (1, field.shape[-1]), jnp.float32)
    upper = jnp.concatenate([flux, zero_row], axis=-2)
    lower = jnp.concatenate([zero_row, flux], axis=-2)
    return field + upper - lower


def deposit(values, cells, rows, cols, width):
    index = cells.astype(jnp.int32)
    span = rows * cols
    channel = index // span
    remain = index % span
    row = remain // cols
    column = channel * cols + remain % cols
    row_hit = (row[:, None] == jnp.arange(rows, dtype=jnp.int32)[None, :]).astype(jnp.bfloat16)
    hit = column[:, None] == jnp.arange(width, dtype=jnp.int32)[None, :]
    rounded = lax.reduce_precision(values, exponent_bits=8, mantissa_bits=7)
    high = rounded.astype(jnp.bfloat16)
    low = (values - rounded).astype(jnp.bfloat16)
    zero = jnp.zeros((), jnp.bfloat16)
    weighted = jnp.concatenate(
        [jnp.where(hit, high[:, None], zero), jnp.where(hit, low[:, None], zero)], axis=1
    )
    both = jnp.einsum("nr,nj->rj", row_hit, weighted, preferred_element_type=jnp.float32)
    return both[:, :width] + both[:, width:]


def exchange(blocks, axis, count):
    me = lax.axis_index(axis)
    out = jnp.zeros_like(blocks)
    out = lax.dynamic_update_index_in_dim(out, lax.dynamic_index_in_dim(blocks, me, 0, keepdims=False), me, 0)
    for s in range(1, count):
        pairs = [(i, i ^ s) for i in range(count)]
        sent = lax.dynamic_index_in_dim(blocks, me ^ s, 0, keepdims=False)
        got = lax.ppermute(sent, axis, pairs)
        out = lax.dynamic_update_index_in_dim(out, got, me ^ s, 0)
    return out


def scatter_sum(x, axis, count):
    blocks = x.reshape((count, x.shape[0] // count) + x.shape[1:])
    return exchange(blocks, axis, count).sum(axis=0)


def gather_blocks(x, axis, count):
    me = lax.axis_index(axis)
    out = jnp.zeros((count,) + x.shape, x.dtype)
    out = lax.dynamic_update_index_in_dim(out, x, me, 0)
    for s in range(1, count):
        pairs = [(i, i ^ s) for i in range(count)]
        out = lax.dynamic_update_index_in_dim(out, lax.ppermute(x, axis, pairs), me ^ s, 0)
    return out.reshape((-1,) + x.shape[1:])


def sweep_kernel(pert_ref, adj_ref, halo_ref, cx_ref, cxh_ref, cy_ref, out_ref):
    kl = pert_ref.shape[0]
    nr, nq = adj_ref.shape[2], adj_ref.shape[3]
    coef = jnp.concatenate([cx_ref[0], cxh_ref[0]], axis=1)
    rows = lax.broadcasted_iota(jnp.int32, (nr, nq), 0)
    north = jnp.where(rows < nr - 1, cy_ref[0], 0.0)
    a0 = adj_ref[0, 0]
    a1 = adj_ref[1, 0]
    acc0 = jnp.zeros((nr, nq), jnp.float32)
    acc1 = jnp.zeros((nr, nq), jnp.float32)
    for k in range(kl):
        p0 = pert_ref[k, 0, 0].astype(jnp.float32)
        p1 = pert_ref[k, 1, 0].astype(jnp.float32)
        v = jnp.concatenate([p0 * a0 + p1 * a1, halo_ref[k, 0]], axis=1)
        for step in range(SWEEPS):
            flux = coef * (pltpu.roll(v, 2 * nq - 1, 1) - v)
            v = v + flux - pltpu.roll(flux, 1, 1)
        v = v[:, :nq]
        for step in range(SWEEPS):
            flux = north * (pltpu.roll(v, nr - 1, 0) - v)
            v = v + flux - pltpu.roll(flux, 1, 0)
        acc0 = acc0 + p0 * v
        acc1 = acc1 + p1 * v
    out_ref[0, 0] = acc0
    out_ref[1, 0] = acc1


def sweeps(perturb, adjoint, halo, coef_x, coef_halo, coef_y, level):
    kl, nf, nl, nr, nq = perturb.shape
    return pl.pallas_call(
        sweep_kernel,
        grid=(1,),
        in_specs=[
            pl.BlockSpec((kl, nf, 1, nr, nq), lambda i: (0, 0, level, 0, 0)),
            pl.BlockSpec((nf, 1, nr, nq), lambda i: (0, level, 0, 0)),
            pl.BlockSpec((kl, 1, nr, nq), lambda i: (0, 0, 0, 0)),
            pl.BlockSpec((1, nr, nq), lambda i: (level, 0, 0)),
            pl.BlockSpec((1, nr, nq), lambda i: (0, 0, 0)),
            pl.BlockSpec((1, nr, nq), lambda i: (level, 0, 0)),
        ],
        out_specs=pl.BlockSpec((nf, 1, nr, nq), lambda i: (0, 0, 0, 0)),
        out_shape=jax.ShapeDtypeStruct((nf, 1, nr, nq), jnp.float32),
    )(perturb, adjoint, halo, coef_x, coef_halo, coef_y)


def on_device(perturb, coef_x, coef_y, obs_values, obs_tile, obs_cell):
    tiles = lax.axis_size("tile")
    mems = lax.axis_size("mem")
    kl, nf, nl, nr, nq = perturb.shape
    members = kl * mems
    width = nf * nl * nq
    halo = SWEEPS

    assert tiles & (tiles - 1) == 0 and mems & (mems - 1) == 0
    forward = [(i, (i + 1) % tiles) for i in range(tiles)]
    backward = [((i + 1) % tiles, i) for i in range(tiles)]

    target = obs_tile[:, 0]
    dest = jnp.arange(tiles, dtype=jnp.int32)[:, None]
    values = jnp.where(target[None, :] == dest, obs_values[None, :], 0.0)
    cells = jnp.broadcast_to(obs_cell.astype(jnp.float32)[None, :], values.shape)
    incoming = exchange(jnp.stack([values, cells], axis=1), "tile", tiles)
    field = deposit(incoming[0, 0], incoming[0, 1], nr, nq, width)
    for source in range(1, tiles):
        field = field + deposit(incoming[source, 0], incoming[source, 1], nr, nq, width)
    field = gather_blocks(scatter_sum(field, "mem", mems), "mem", mems)
    adjoint = jnp.transpose(field.reshape(nr, nf, nl, nq), (1, 2, 0, 3))

    widened = perturb.astype(jnp.float32)
    pieces = []
    for level in range(nl):
        here = widened[:, :, level]
        low_edge = jnp.sum(here[..., :halo] * adjoint[None, :, level, :, :halo], axis=1)
        high_edge = jnp.sum(here[..., -halo:] * adjoint[None, :, level, :, -halo:], axis=1)
        left = lax.ppermute(
            jnp.concatenate([high_edge, coef_x[None, level, :, -halo:]], axis=0), "tile", forward
        )
        right = lax.ppermute(
            jnp.concatenate([low_edge, coef_x[None, level, :, :halo]], axis=0), "tile", backward
        )
        gap = jnp.zeros(left.shape[:-1] + (nq - 2 * halo,), jnp.float32)
        ring = jnp.concatenate([right, gap, left], axis=-1)[:, None]
        part = sweeps(perturb, adjoint, ring[:-1], coef_x, ring[-1], coef_y, level)
        blocks = jnp.transpose(part.reshape((nf, mems, nr // mems, nq)), (1, 0, 2, 3))
        pieces.append(exchange(blocks, "mem", mems).sum(axis=0))
    summed = jnp.transpose(jnp.stack(pieces, axis=1), (2, 0, 1, 3))
    return summed / (members - 1)


def solution(mesh):
    return jax.shard_map(
        on_device,
        mesh=mesh,
        in_specs=(
            P("mem", None, None, None, "tile"),
            P(None, None, "tile"),
            P(None, None, "tile"),
            P(("mem", "tile")),
            P(("mem", "tile"), None),
            P(("mem", "tile")),
        ),
        out_specs=P("mem", None, None, "tile"),
        check_vma=False,
    )
```

```python
import jax
import jax.numpy as jnp
from jax import lax
from jax.sharding import PartitionSpec as P

FIELDS = 2
LEVELS = 2
SWEEPS = 6
LAT = 256


def sweep_north(field, coef):
    flux = coef[..., :-1, :] * (field[..., 1:, :] - field[..., :-1, :])
    zero_row = jnp.zeros(field.shape[:-2] + (1, field.shape[-1]), jnp.float32)
    upper = jnp.concatenate([flux, zero_row], axis=-2)
    lower = jnp.concatenate([zero_row, flux], axis=-2)
    return field + upper - lower


def deposit(values, cells, rows, cols, width):
    index = cells.astype(jnp.int32)
    span = rows * cols
    channel = index // span
    remain = index % span
    row = remain // cols
    column = channel * cols + remain % cols
    row_hit = (row[:, None] == jnp.arange(rows, dtype=jnp.int32)[None, :]).astype(jnp.bfloat16)
    hit = column[:, None] == jnp.arange(width, dtype=jnp.int32)[None, :]
    rounded = lax.reduce_precision(values, exponent_bits=8, mantissa_bits=7)
    high = rounded.astype(jnp.bfloat16)
    low = (values - rounded).astype(jnp.bfloat16)
    zero = jnp.zeros((), jnp.bfloat16)
    weighted = jnp.concatenate(
        [jnp.where(hit, high[:, None], zero), jnp.where(hit, low[:, None], zero)], axis=1
    )
    both = jnp.einsum("nr,nj->rj", row_hit, weighted, preferred_element_type=jnp.float32)
    return both[:, :width] + both[:, width:]


def exchange(blocks, axis, count):
    me = lax.axis_index(axis)
    out = jnp.zeros_like(blocks)
    out = lax.dynamic_update_index_in_dim(out, lax.dynamic_index_in_dim(blocks, me, 0, keepdims=False), me, 0)
    for s in range(1, count):
        pairs = [(i, i ^ s) for i in range(count)]
        sent = lax.dynamic_index_in_dim(blocks, me ^ s, 0, keepdims=False)
        got = lax.ppermute(sent, axis, pairs)
        out = lax.dynamic_update_index_in_dim(out, got, me ^ s, 0)
    return out


def scatter_sum(x, axis, count):
    blocks = x.reshape((count, x.shape[0] // count) + x.shape[1:])
    return exchange(blocks, axis, count).sum(axis=0)


def gather_blocks(x, axis, count):
    me = lax.axis_index(axis)
    out = jnp.zeros((count,) + x.shape, x.dtype)
    out = lax.dynamic_update_index_in_dim(out, x, me, 0)
    for s in range(1, count):
        pairs = [(i, i ^ s) for i in range(count)]
        out = lax.dynamic_update_index_in_dim(out, lax.ppermute(x, axis, pairs), me ^ s, 0)
    return out.reshape((-1,) + x.shape[1:])


def on_device(perturb, coef_x, coef_y, obs_values, obs_tile, obs_cell):
    tiles = lax.axis_size("tile")
    mems = lax.axis_size("mem")
    kl, nf, nl, nr, nq = perturb.shape
    members = kl * mems
    width = nf * nl * nq
    halo = SWEEPS

    assert tiles & (tiles - 1) == 0 and mems & (mems - 1) == 0
    forward = [(i, (i + 1) % tiles) for i in range(tiles)]
    backward = [((i + 1) % tiles, i) for i in range(tiles)]

    target = obs_tile[:, 0]
    dest = jnp.arange(tiles, dtype=jnp.int32)[:, None]
    values = jnp.where(target[None, :] == dest, obs_values[None, :], 0.0)
    cells = jnp.broadcast_to(obs_cell.astype(jnp.float32)[None, :], values.shape)
    outgoing = jnp.stack([values, cells], axis=1)
    me = lax.axis_index("tile")
    own = lax.dynamic_index_in_dim(outgoing, me, 0, keepdims=False)
    field = deposit(own[0], own[1], nr, nq, width)
    for s in range(1, tiles):
        pairs = [(i, i ^ s) for i in range(tiles)]
        sent = lax.dynamic_index_in_dim(outgoing, me ^ s, 0, keepdims=False)
        got = lax.ppermute(sent, "tile", pairs)
        field = field + deposit(got[0], got[1], nr, nq, width)
    field = gather_blocks(scatter_sum(field, "mem", mems), "mem", mems)
    adjoint = jnp.transpose(field.reshape(nr, nf, nl, nq), (1, 2, 0, 3))

    widened = perturb.astype(jnp.float32)
    product = jnp.sum(widened * adjoint[None], axis=1)
    joined = jnp.concatenate([product, coef_x[None]], axis=0)
    left = lax.ppermute(joined[..., -halo:], "tile", forward)
    right = lax.ppermute(joined[..., :halo], "tile", backward)
    joined = jnp.concatenate([left, joined, right], axis=-1)
    value, coef = joined[:-1], joined[-1]
    for step in range(SWEEPS):
        flux = coef[..., :-1] * (value[..., 1:] - value[..., :-1])
        value = value[..., 1:-1] + flux[..., 1:] - flux[..., :-1]
        coef = coef[..., 1:-1]
    product = value
    for step in range(SWEEPS):
        product = sweep_north(product, coef_y)
    part = jnp.einsum("kflyx,klyx->yflx", widened, product)
    summed = scatter_sum(part, "mem", mems)
    return summed / (members - 1)


def solution(mesh):
    return jax.shard_map(
        on_device,
        mesh=mesh,
        in_specs=(
            P("mem", None, None, None, "tile"),
            P(None, None, "tile"),
            P(None, None, "tile"),
            P(("mem", "tile")),
            P(("mem", "tile"), None),
            P(("mem", "tile")),
        ),
        out_specs=P("mem", None, None, "tile"),
        check_vma=False,
    )
```

```python
import jax
import jax.numpy as jnp
from jax import lax
from jax.sharding import PartitionSpec as P

FIELDS = 2
LEVELS = 2
SWEEPS = 6
LAT = 256


def sweep_north(field, coef):
    flux = coef[..., :-1, :] * (field[..., 1:, :] - field[..., :-1, :])
    zero_row = jnp.zeros(field.shape[:-2] + (1, field.shape[-1]), jnp.float32)
    upper = jnp.concatenate([flux, zero_row], axis=-2)
    lower = jnp.concatenate([zero_row, flux], axis=-2)
    return field + upper - lower


def deposit(values, cells, rows, cols, width):
    index = cells.astype(jnp.int32)
    span = rows * cols
    channel = index // span
    remain = index % span
    row = remain // cols
    column = channel * cols + remain % cols
    row_hit = (row[:, None] == jnp.arange(rows, dtype=jnp.int32)[None, :]).astype(jnp.bfloat16)
    hit = column[:, None] == jnp.arange(width, dtype=jnp.int32)[None, :]
    rounded = lax.reduce_precision(values, exponent_bits=8, mantissa_bits=7)
    high = rounded.astype(jnp.bfloat16)
    low = (values - rounded).astype(jnp.bfloat16)
    zero = jnp.zeros((), jnp.bfloat16)
    weighted = jnp.concatenate(
        [jnp.where(hit, high[:, None], zero), jnp.where(hit, low[:, None], zero)], axis=1
    )
    both = jnp.einsum("nr,nj->rj", row_hit, weighted, preferred_element_type=jnp.float32)
    return both[:, :width] + both[:, width:]


def exchange(blocks, axis, count):
    me = lax.axis_index(axis)
    out = jnp.zeros_like(blocks)
    out = lax.dynamic_update_index_in_dim(out, lax.dynamic_index_in_dim(blocks, me, 0, keepdims=False), me, 0)
    for s in range(1, count):
        pairs = [(i, i ^ s) for i in range(count)]
        sent = lax.dynamic_index_in_dim(blocks, me ^ s, 0, keepdims=False)
        got = lax.ppermute(sent, axis, pairs)
        out = lax.dynamic_update_index_in_dim(out, got, me ^ s, 0)
    return out


def scatter_sum(x, axis, count):
    blocks = x.reshape((count, x.shape[0] // count) + x.shape[1:])
    return exchange(blocks, axis, count).sum(axis=0)


def gather_blocks(x, axis, count):
    me = lax.axis_index(axis)
    out = jnp.zeros((count,) + x.shape, x.dtype)
    out = lax.dynamic_update_index_in_dim(out, x, me, 0)
    for s in range(1, count):
        pairs = [(i, i ^ s) for i in range(count)]
        out = lax.dynamic_update_index_in_dim(out, lax.ppermute(x, axis, pairs), me ^ s, 0)
    return out.reshape((-1,) + x.shape[1:])


def on_device(perturb, coef_x, coef_y, obs_values, obs_tile, obs_cell):
    tiles = lax.axis_size("tile")
    mems = lax.axis_size("mem")
    kl, nf, nl, nr, nq = perturb.shape
    members = kl * mems
    width = nf * nl * nq
    halo = SWEEPS

    assert tiles & (tiles - 1) == 0 and mems & (mems - 1) == 0
    forward = [(i, (i + 1) % tiles) for i in range(tiles)]
    backward = [((i + 1) % tiles, i) for i in range(tiles)]

    target = obs_tile[:, 0]
    dest = jnp.arange(tiles, dtype=jnp.int32)[:, None]
    values = jnp.where(target[None, :] == dest, obs_values[None, :], 0.0)
    cells = jnp.broadcast_to(obs_cell.astype(jnp.float32)[None, :], values.shape)
    outgoing = jnp.stack([values, cells], axis=1)
    me = lax.axis_index("tile")
    own = lax.dynamic_index_in_dim(outgoing, me, 0, keepdims=False)
    field = deposit(own[0], own[1], nr, nq, width)
    for s in range(1, tiles):
        pairs = [(i, i ^ s) for i in range(tiles)]
        sent = lax.dynamic_index_in_dim(outgoing, me ^ s, 0, keepdims=False)
        got = lax.ppermute(sent, "tile", pairs)
        field = field + deposit(got[0], got[1], nr, nq, width)
    field = gather_blocks(scatter_sum(field, "mem", mems), "mem", mems)
    adjoint = jnp.transpose(field.reshape(nr, nf, nl, nq), (1, 2, 0, 3))

    widened = perturb.astype(jnp.float32)
    low_edge = jnp.sum(widened[..., :halo] * adjoint[None, ..., :halo], axis=1)
    high_edge = jnp.sum(widened[..., -halo:] * adjoint[None, ..., -halo:], axis=1)
    left = lax.ppermute(
        jnp.concatenate([high_edge, coef_x[None, ..., -halo:]], axis=0), "tile", forward
    )
    right = lax.ppermute(
        jnp.concatenate([low_edge, coef_x[None, ..., :halo]], axis=0), "tile", backward
    )
    product = jnp.sum(widened * adjoint[None], axis=1)
    value = jnp.concatenate([left[:-1], product, right[:-1]], axis=-1)
    coef = jnp.concatenate([left[-1], coef_x, right[-1]], axis=-1)
    for step in range(SWEEPS):
        east = coef[..., 1:-1] * (value[..., 2:] - value[..., 1:-1])
        west = coef[..., :-2] * (value[..., 1:-1] - value[..., :-2])
        value = value[..., 1:-1] + east - west
        coef = coef[..., 1:-1]
    product = value
    for step in range(SWEEPS):
        product = sweep_north(product, coef_y)
    part = jnp.einsum("kflyx,klyx->yflx", widened, product)
    summed = scatter_sum(part, "mem", mems)
    return summed / (members - 1)


def solution(mesh):
    return jax.shard_map(
        on_device,
        mesh=mesh,
        in_specs=(
            P("mem", None, None, None, "tile"),
            P(None, None, "tile"),
            P(None, None, "tile"),
            P(("mem", "tile")),
            P(("mem", "tile"), None),
            P(("mem", "tile")),
        ),
        out_specs=P("mem", None, None, "tile"),
        check_vma=False,
    )
```

```python
import jax
import jax.numpy as jnp
from jax import lax
from jax.experimental import pallas as pl
from jax.experimental.pallas import tpu as pltpu
from jax.sharding import PartitionSpec as P

FIELDS = 2
LEVELS = 2
SWEEPS = 6
LAT = 256


def sweep_north(field, coef):
    flux = coef[..., :-1, :] * (field[..., 1:, :] - field[..., :-1, :])
    zero_row = jnp.zeros(field.shape[:-2] + (1, field.shape[-1]), jnp.float32)
    upper = jnp.concatenate([flux, zero_row], axis=-2)
    lower = jnp.concatenate([zero_row, flux], axis=-2)
    return field + upper - lower


def deposit(values, cells, rows, width):
    index = cells.astype(jnp.int32)
    row = index // width
    column = index % width
    row_hit = (row[:, None] == jnp.arange(rows, dtype=jnp.int32)[None, :]).astype(jnp.bfloat16)
    hit = column[:, None] == jnp.arange(width, dtype=jnp.int32)[None, :]
    rounded = lax.reduce_precision(values, exponent_bits=8, mantissa_bits=7)
    high = rounded.astype(jnp.bfloat16)
    low = (values - rounded).astype(jnp.bfloat16)
    zero = jnp.zeros((), jnp.bfloat16)
    weighted = jnp.concatenate(
        [jnp.where(hit, high[:, None], zero), jnp.where(hit, low[:, None], zero)], axis=1
    )
    both = jnp.einsum("nr,nj->rj", row_hit, weighted, preferred_element_type=jnp.float32)
    return both[:, :width] + both[:, width:]


def exchange(blocks, axis, count):
    me = lax.axis_index(axis)
    out = jnp.zeros_like(blocks)
    out = lax.dynamic_update_index_in_dim(out, lax.dynamic_index_in_dim(blocks, me, 0, keepdims=False), me, 0)
    for s in range(1, count):
        pairs = [(i, i ^ s) for i in range(count)]
        sent = lax.dynamic_index_in_dim(blocks, me ^ s, 0, keepdims=False)
        got = lax.ppermute(sent, axis, pairs)
        out = lax.dynamic_update_index_in_dim(out, got, me ^ s, 0)
    return out


def scatter_sum(x, axis, count):
    blocks = x.reshape((count, x.shape[0] // count) + x.shape[1:])
    return exchange(blocks, axis, count).sum(axis=0)


def gather_blocks(x, axis, count):
    me = lax.axis_index(axis)
    out = jnp.zeros((count,) + x.shape, x.dtype)
    out = lax.dynamic_update_index_in_dim(out, x, me, 0)
    for s in range(1, count):
        pairs = [(i, i ^ s) for i in range(count)]
        out = lax.dynamic_update_index_in_dim(out, lax.ppermute(x, axis, pairs), me ^ s, 0)
    return out.reshape((-1,) + x.shape[1:])


def sweep_kernel(pert_ref, adj_ref, halo_ref, cx_ref, cxh_ref, cy_ref, out_ref):
    kl = pert_ref.shape[0]
    nr, nq = adj_ref.shape[2], adj_ref.shape[3]
    span = nq + halo_ref.shape[2]
    coef = jnp.concatenate([cx_ref[0].T, cxh_ref[0]], axis=0)
    rows = lax.broadcasted_iota(jnp.int32, (nr, nq), 0)
    north = jnp.where(rows < nr - 1, cy_ref[0], 0.0)
    a0 = adj_ref[0, 0]
    a1 = adj_ref[1, 0]
    acc0 = jnp.zeros((nr, nq), jnp.float32)
    acc1 = jnp.zeros((nr, nq), jnp.float32)
    for k in range(kl):
        p0 = pert_ref[k, 0, 0].astype(jnp.float32)
        p1 = pert_ref[k, 1, 0].astype(jnp.float32)
        v = jnp.concatenate([(p0 * a0 + p1 * a1).T, halo_ref[k, 0]], axis=0)
        for step in range(SWEEPS):
            flux = coef * (pltpu.roll(v, span - 1, 0) - v)
            v = v + flux - pltpu.roll(flux, 1, 0)
        v = v[:nq].T
        for step in range(SWEEPS):
            flux = north * (pltpu.roll(v, nr - 1, 0) - v)
            v = v + flux - pltpu.roll(flux, 1, 0)
        acc0 = acc0 + p0 * v
        acc1 = acc1 + p1 * v
    out_ref[0, 0] = acc0
    out_ref[1, 0] = acc1


def turned(ring, halo):
    pad = -(-2 * halo // 8) * 8
    gap = jnp.zeros(ring.shape[:-1] + (pad - 2 * halo,), ring.dtype)
    block = jnp.concatenate([ring[..., :halo], gap, ring[..., -halo:]], axis=-1)
    return jnp.swapaxes(block, -1, -2)


def sweeps(perturb, adjoint, halo, coef_x, coef_halo, coef_y):
    kl, nf, nl, nr, nq = perturb.shape
    pad = halo.shape[2]
    return pl.pallas_call(
        sweep_kernel,
        grid=(nl,),
        in_specs=[
            pl.BlockSpec((kl, nf, 1, nr, nq), lambda l: (0, 0, l, 0, 0)),
            pl.BlockSpec((nf, 1, nr, nq), lambda l: (0, l, 0, 0)),
            pl.BlockSpec((kl, 1, pad, nr), lambda l: (0, l, 0, 0)),
            pl.BlockSpec((1, nr, nq), lambda l: (l, 0, 0)),
            pl.BlockSpec((1, pad, nr), lambda l: (l, 0, 0)),
            pl.BlockSpec((1, nr, nq), lambda l: (l, 0, 0)),
        ],
        out_specs=pl.BlockSpec((nf, 1, nr, nq), lambda l: (0, l, 0, 0)),
        out_shape=jax.ShapeDtypeStruct((nf, nl, nr, nq), jnp.float32),
    )(perturb, adjoint, halo, coef_x, coef_halo, coef_y)


def on_device(perturb, coef_x, coef_y, obs_values, obs_tile, obs_cell):
    tiles = lax.axis_size("tile")
    mems = lax.axis_size("mem")
    kl, nf, nl, nr, nq = perturb.shape
    members = kl * mems
    halo = SWEEPS
    group = 32
    main = nf * nl * nq
    width = main + 128
    assert tiles >= 3 and tiles & (tiles - 1) == 0 and mems & (mems - 1) == 0
    assert nf * nl * group <= 128 and 2 * halo <= group
    forward = [(i, (i + 1) % tiles) for i in range(tiles)]
    backward = [((i + 1) % tiles, i) for i in range(tiles)]

    widened = perturb.astype(jnp.float32)
    edges = jnp.concatenate([widened.reshape((kl * nf * nl, nr, nq)), coef_x], axis=0)
    from_left = lax.ppermute(edges[..., -halo:], "tile", forward)
    from_right = lax.ppermute(edges[..., :halo], "tile", backward)

    target = obs_tile[:, 0]
    line = obs_cell // nq
    channel = line // nr
    row = line % nr
    column = obs_cell % nq
    dest = jnp.arange(tiles, dtype=jnp.int32)[:, None]
    apart = (target[None, :] - dest) % tiles
    home = channel * nq + column
    lower = main + channel * group + column
    upper = main + channel * group + group - nq + column
    place = jnp.where(apart == 0, home[None, :], jnp.where(apart == 1, lower[None, :], upper[None, :]))
    inside = (apart == 0) | ((apart == 1) & (column[None, :] < halo)) | (
        (apart == tiles - 1) & (column[None, :] >= nq - halo)
    )
    values = jnp.where(inside, obs_values[None, :], 0.0)
    cells = jnp.where(inside, row[None, :] * width + place, 0).astype(jnp.float32)
    outgoing = jnp.stack([values, cells], axis=1)
    me = lax.axis_index("tile")
    own = lax.dynamic_index_in_dim(outgoing, me, 0, keepdims=False)
    field = deposit(own[0], own[1], nr, width)
    for s in range(1, tiles):
        pairs = [(i, i ^ s) for i in range(tiles)]
        sent = lax.dynamic_index_in_dim(outgoing, me ^ s, 0, keepdims=False)
        got = lax.ppermute(sent, "tile", pairs)
        field = field + deposit(got[0], got[1], nr, width)
    field = gather_blocks(scatter_sum(field, "mem", mems), "mem", mems)
    adjoint = jnp.transpose(field[:, :main].reshape(nr, nf, nl, nq), (1, 2, 0, 3))
    rim = jnp.transpose(field[:, main:].reshape(nr, nf, nl, group), (1, 2, 0, 3))

    count = kl * nf * nl
    left_p = from_left[:count].reshape((kl, nf, nl, nr, halo))
    right_p = from_right[:count].reshape((kl, nf, nl, nr, halo))
    left = jnp.sum(left_p * rim[None, ..., group - halo:], axis=1)
    right = jnp.sum(right_p * rim[None, ..., :halo], axis=1)
    pad = -(-2 * halo // 8) * 8
    gap = jnp.zeros(left.shape[:-1] + (pad - 2 * halo,), jnp.float32)
    ring = jnp.swapaxes(jnp.concatenate([right, gap, left], axis=-1), -1, -2)
    cgap = jnp.zeros((nl, nr, pad - 2 * halo), jnp.float32)
    cring = jnp.swapaxes(jnp.concatenate([from_right[count:], cgap, from_left[count:]], axis=-1), -1, -2)
    part = sweeps(perturb, adjoint, ring, coef_x, cring, coef_y)
    blocks = part.reshape((nf, nl, mems, nr // mems, nq))
    blocks = jnp.transpose(blocks, (2, 0, 1, 3, 4))
    summed = jnp.transpose(exchange(blocks, "mem", mems).sum(axis=0), (2, 0, 1, 3))
    return summed / (members - 1)


def solution(mesh):
    return jax.shard_map(
        on_device,
        mesh=mesh,
        in_specs=(
            P("mem", None, None, None, "tile"),
            P(None, None, "tile"),
            P(None, None, "tile"),
            P(("mem", "tile")),
            P(("mem", "tile"), None),
            P(("mem", "tile")),
        ),
        out_specs=P("mem", None, None, "tile"),
        check_vma=False,
    )
```

```python
import jax
import jax.numpy as jnp
from jax import lax
from jax.experimental import pallas as pl
from jax.experimental.pallas import tpu as pltpu
from jax.sharding import PartitionSpec as P

FIELDS = 2
LEVELS = 2
SWEEPS = 6
LAT = 256


def sweep_north(field, coef):
    flux = coef[..., :-1, :] * (field[..., 1:, :] - field[..., :-1, :])
    zero_row = jnp.zeros(field.shape[:-2] + (1, field.shape[-1]), jnp.float32)
    upper = jnp.concatenate([flux, zero_row], axis=-2)
    lower = jnp.concatenate([zero_row, flux], axis=-2)
    return field + upper - lower


def deposit(values, cells, rows, width):
    index = cells.astype(jnp.int32)
    row = index // width
    column = index % width
    row_hit = row[:, None] == jnp.arange(rows, dtype=jnp.int32)[None, :]
    hit = (column[:, None] == jnp.arange(width, dtype=jnp.int32)[None, :]).astype(jnp.bfloat16)
    rounded = lax.reduce_precision(values, exponent_bits=8, mantissa_bits=7)
    high = rounded.astype(jnp.bfloat16)
    low = (values - rounded).astype(jnp.bfloat16)
    zero = jnp.zeros((), jnp.bfloat16)
    weighted = jnp.concatenate(
        [jnp.where(row_hit, high[:, None], zero), jnp.where(row_hit, low[:, None], zero)], axis=1
    )
    both = jnp.einsum("nr,nj->rj", weighted, hit, preferred_element_type=jnp.float32)
    return both[:rows] + both[rows:]


def exchange(blocks, axis, count):
    me = lax.axis_index(axis)
    out = jnp.zeros_like(blocks)
    out = lax.dynamic_update_index_in_dim(out, lax.dynamic_index_in_dim(blocks, me, 0, keepdims=False), me, 0)
    for s in range(1, count):
        pairs = [(i, i ^ s) for i in range(count)]
        sent = lax.dynamic_index_in_dim(blocks, me ^ s, 0, keepdims=False)
        got = lax.ppermute(sent, axis, pairs)
        out = lax.dynamic_update_index_in_dim(out, got, me ^ s, 0)
    return out


def scatter_sum(x, axis, count):
    blocks = x.reshape((count, x.shape[0] // count) + x.shape[1:])
    return exchange(blocks, axis, count).sum(axis=0)


def gather_blocks(x, axis, count):
    me = lax.axis_index(axis)
    out = jnp.zeros((count,) + x.shape, x.dtype)
    out = lax.dynamic_update_index_in_dim(out, x, me, 0)
    for s in range(1, count):
        pairs = [(i, i ^ s) for i in range(count)]
        out = lax.dynamic_update_index_in_dim(out, lax.ppermute(x, axis, pairs), me ^ s, 0)
    return out.reshape((-1,) + x.shape[1:])


def sweep_kernel(pert_ref, adj_ref, halo_ref, cx_ref, cxh_ref, cy_ref, out_ref):
    kl = pert_ref.shape[0]
    nr, nq = adj_ref.shape[2], adj_ref.shape[3]
    span = nq + halo_ref.shape[2]
    coef = jnp.concatenate([cx_ref[0].T, cxh_ref[0]], axis=0)
    rows = lax.broadcasted_iota(jnp.int32, (nr, nq), 0)
    north = jnp.where(rows < nr - 1, cy_ref[0], 0.0)
    a0 = adj_ref[0, 0]
    a1 = adj_ref[1, 0]
    acc0 = jnp.zeros((nr, nq), jnp.float32)
    acc1 = jnp.zeros((nr, nq), jnp.float32)
    for k in range(kl):
        p0 = pert_ref[k, 0, 0].astype(jnp.float32)
        p1 = pert_ref[k, 1, 0].astype(jnp.float32)
        v = jnp.concatenate([(p0 * a0 + p1 * a1).T, halo_ref[k, 0]], axis=0)
        for step in range(SWEEPS):
            flux = coef * (pltpu.roll(v, span - 1, 0) - v)
            v = v + flux - pltpu.roll(flux, 1, 0)
        v = v[:nq].T
        for step in range(SWEEPS):
            flux = north * (pltpu.roll(v, nr - 1, 0) - v)
            v = v + flux - pltpu.roll(flux, 1, 0)
        acc0 = acc0 + p0 * v
        acc1 = acc1 + p1 * v
    out_ref[0, 0] = acc0
    out_ref[1, 0] = acc1


def turned(ring, halo):
    pad = -(-2 * halo // 8) * 8
    gap = jnp.zeros(ring.shape[:-1] + (pad - 2 * halo,), ring.dtype)
    block = jnp.concatenate([ring[..., :halo], gap, ring[..., -halo:]], axis=-1)
    return jnp.swapaxes(block, -1, -2)


def sweeps(perturb, adjoint, halo, coef_x, coef_halo, coef_y):
    kl, nf, nl, nr, nq = perturb.shape
    pad = halo.shape[2]
    return pl.pallas_call(
        sweep_kernel,
        grid=(nl,),
        in_specs=[
            pl.BlockSpec((kl, nf, 1, nr, nq), lambda l: (0, 0, l, 0, 0)),
            pl.BlockSpec((nf, 1, nr, nq), lambda l: (0, l, 0, 0)),
            pl.BlockSpec((kl, 1, pad, nr), lambda l: (0, l, 0, 0)),
            pl.BlockSpec((1, nr, nq), lambda l: (l, 0, 0)),
            pl.BlockSpec((1, pad, nr), lambda l: (l, 0, 0)),
            pl.BlockSpec((1, nr, nq), lambda l: (l, 0, 0)),
        ],
        out_specs=pl.BlockSpec((nf, 1, nr, nq), lambda l: (0, l, 0, 0)),
        out_shape=jax.ShapeDtypeStruct((nf, nl, nr, nq), jnp.float32),
    )(perturb, adjoint, halo, coef_x, coef_halo, coef_y)


def on_device(perturb, coef_x, coef_y, obs_values, obs_tile, obs_cell):
    tiles = lax.axis_size("tile")
    mems = lax.axis_size("mem")
    kl, nf, nl, nr, nq = perturb.shape
    members = kl * mems
    halo = SWEEPS
    group = 32
    main = nf * nl * nq
    width = main + 128
    assert tiles >= 3 and tiles & (tiles - 1) == 0 and mems & (mems - 1) == 0
    assert nf * nl * group <= 128 and 2 * halo <= group
    forward = [(i, (i + 1) % tiles) for i in range(tiles)]
    backward = [((i + 1) % tiles, i) for i in range(tiles)]

    widened = perturb.astype(jnp.float32)
    edges = jnp.concatenate([widened.reshape((kl * nf * nl, nr, nq)), coef_x], axis=0)
    from_left = lax.ppermute(edges[..., -halo:], "tile", forward)
    from_right = lax.ppermute(edges[..., :halo], "tile", backward)

    target = obs_tile[:, 0]
    line = obs_cell // nq
    channel = line // nr
    row = line % nr
    column = obs_cell % nq
    dest = jnp.arange(tiles, dtype=jnp.int32)[:, None]
    apart = (target[None, :] - dest) % tiles
    home = channel * nq + column
    lower = main + channel * group + column
    upper = main + channel * group + group - nq + column
    place = jnp.where(apart == 0, home[None, :], jnp.where(apart == 1, lower[None, :], upper[None, :]))
    inside = (apart == 0) | ((apart == 1) & (column[None, :] < halo)) | (
        (apart == tiles - 1) & (column[None, :] >= nq - halo)
    )
    values = jnp.where(inside, obs_values[None, :], 0.0)
    cells = jnp.where(inside, row[None, :] * width + place, 0).astype(jnp.float32)
    outgoing = jnp.stack([values, cells], axis=1)
    me = lax.axis_index("tile")
    own = lax.dynamic_index_in_dim(outgoing, me, 0, keepdims=False)
    field = deposit(own[0], own[1], nr, width)
    for s in range(1, tiles):
        pairs = [(i, i ^ s) for i in range(tiles)]
        sent = lax.dynamic_index_in_dim(outgoing, me ^ s, 0, keepdims=False)
        got = lax.ppermute(sent, "tile", pairs)
        field = field + deposit(got[0], got[1], nr, width)
    field = gather_blocks(scatter_sum(field, "mem", mems), "mem", mems)
    adjoint = jnp.transpose(field[:, :main].reshape(nr, nf, nl, nq), (1, 2, 0, 3))
    rim = jnp.transpose(field[:, main:].reshape(nr, nf, nl, group), (1, 2, 0, 3))

    count = kl * nf * nl
    left_p = from_left[:count].reshape((kl, nf, nl, nr, halo))
    right_p = from_right[:count].reshape((kl, nf, nl, nr, halo))
    left = jnp.sum(left_p * rim[None, ..., group - halo:], axis=1)
    right = jnp.sum(right_p * rim[None, ..., :halo], axis=1)
    pad = -(-2 * halo // 8) * 8
    gap = jnp.zeros(left.shape[:-1] + (pad - 2 * halo,), jnp.float32)
    ring = jnp.swapaxes(jnp.concatenate([right, gap, left], axis=-1), -1, -2)
    cgap = jnp.zeros((nl, nr, pad - 2 * halo), jnp.float32)
    cring = jnp.swapaxes(jnp.concatenate([from_right[count:], cgap, from_left[count:]], axis=-1), -1, -2)
    part = sweeps(perturb, adjoint, ring, coef_x, cring, coef_y)
    blocks = part.reshape((nf, nl, mems, nr // mems, nq))
    blocks = jnp.transpose(blocks, (2, 0, 1, 3, 4))
    summed = jnp.transpose(exchange(blocks, "mem", mems).sum(axis=0), (2, 0, 1, 3))
    return summed / (members - 1)


def solution(mesh):
    return jax.shard_map(
        on_device,
        mesh=mesh,
        in_specs=(
            P("mem", None, None, None, "tile"),
            P(None, None, "tile"),
            P(None, None, "tile"),
            P(("mem", "tile")),
            P(("mem", "tile"), None),
            P(("mem", "tile")),
        ),
        out_specs=P("mem", None, None, "tile"),
        check_vma=False,
    )
```

```python
import jax
import jax.numpy as jnp
from jax import lax
from jax.experimental import pallas as pl
from jax.experimental.pallas import tpu as pltpu
from jax.sharding import PartitionSpec as P

FIELDS = 2
LEVELS = 2
SWEEPS = 6
LAT = 256


def sweep_north(field, coef):
    flux = coef[..., :-1, :] * (field[..., 1:, :] - field[..., :-1, :])
    zero_row = jnp.zeros(field.shape[:-2] + (1, field.shape[-1]), jnp.float32)
    upper = jnp.concatenate([flux, zero_row], axis=-2)
    lower = jnp.concatenate([zero_row, flux], axis=-2)
    return field + upper - lower


def deposit(values, cells, rows, width):
    index = cells.astype(jnp.int32)
    row = index // width
    column = index % width
    row_hit = (row[:, None] == jnp.arange(rows, dtype=jnp.int32)[None, :]).astype(jnp.bfloat16)
    hit = column[:, None] == jnp.arange(width, dtype=jnp.int32)[None, :]
    rounded = lax.reduce_precision(values, exponent_bits=8, mantissa_bits=7)
    high = rounded.astype(jnp.bfloat16)
    low = (values - rounded).astype(jnp.bfloat16)
    zero = jnp.zeros((), jnp.bfloat16)
    weighted = jnp.concatenate(
        [jnp.where(hit, high[:, None], zero), jnp.where(hit, low[:, None], zero)], axis=1
    )
    both = jnp.einsum("nr,nj->rj", row_hit, weighted, preferred_element_type=jnp.float32)
    return both[:, :width] + both[:, width:]


def exchange(blocks, axis, count):
    me = lax.axis_index(axis)
    out = jnp.zeros_like(blocks)
    out = lax.dynamic_update_index_in_dim(out, lax.dynamic_index_in_dim(blocks, me, 0, keepdims=False), me, 0)
    for s in range(1, count):
        pairs = [(i, i ^ s) for i in range(count)]
        sent = lax.dynamic_index_in_dim(blocks, me ^ s, 0, keepdims=False)
        got = lax.ppermute(sent, axis, pairs)
        out = lax.dynamic_update_index_in_dim(out, got, me ^ s, 0)
    return out


def scatter_sum(x, axis, count):
    blocks = x.reshape((count, x.shape[0] // count) + x.shape[1:])
    return exchange(blocks, axis, count).sum(axis=0)


def halving_sum(blocks, axis, count):
    bits = count.bit_length() - 1
    me = lax.axis_index(axis)
    blocks = blocks.reshape((2,) * bits + blocks.shape[1:])
    for b in range(bits):
        pos = bits - 1 - b
        mine = (me >> b) & 1
        keep = lax.dynamic_index_in_dim(blocks, mine, pos, keepdims=False)
        send = lax.dynamic_index_in_dim(blocks, 1 - mine, pos, keepdims=False)
        pairs = [(i, i ^ (1 << b)) for i in range(count)]
        blocks = keep + lax.ppermute(send, axis, pairs)
    return blocks


def gather_blocks(x, axis, count):
    me = lax.axis_index(axis)
    out = jnp.zeros((count,) + x.shape, x.dtype)
    out = lax.dynamic_update_index_in_dim(out, x, me, 0)
    for s in range(1, count):
        pairs = [(i, i ^ s) for i in range(count)]
        out = lax.dynamic_update_index_in_dim(out, lax.ppermute(x, axis, pairs), me ^ s, 0)
    return out.reshape((-1,) + x.shape[1:])


def sweep_kernel(pert_ref, adj_ref, halo_ref, cx_ref, cxh_ref, cy_ref, out_ref):
    kl = pert_ref.shape[0]
    nr, nq = adj_ref.shape[2], adj_ref.shape[3]
    span = nq + halo_ref.shape[2]
    coef = jnp.concatenate([cx_ref[0].T, cxh_ref[0]], axis=0)
    rows = lax.broadcasted_iota(jnp.int32, (nr, nq), 0)
    north = jnp.where(rows < nr - 1, cy_ref[0], 0.0)
    a0 = adj_ref[0, 0]
    a1 = adj_ref[1, 0]
    acc0 = jnp.zeros((nr, nq), jnp.float32)
    acc1 = jnp.zeros((nr, nq), jnp.float32)
    for k in range(kl):
        p0 = pert_ref[k, 0, 0].astype(jnp.float32)
        p1 = pert_ref[k, 1, 0].astype(jnp.float32)
        v = jnp.concatenate([(p0 * a0 + p1 * a1).T, halo_ref[k, 0]], axis=0)
        for step in range(SWEEPS):
            flux = coef * (pltpu.roll(v, span - 1, 0) - v)
            v = v + flux - pltpu.roll(flux, 1, 0)
        v = v[:nq].T
        for step in range(SWEEPS):
            flux = north * (pltpu.roll(v, nr - 1, 0) - v)
            v = v + flux - pltpu.roll(flux, 1, 0)
        acc0 = acc0 + p0 * v
        acc1 = acc1 + p1 * v
    out_ref[0, 0] = acc0
    out_ref[1, 0] = acc1


def turned(ring, halo):
    pad = -(-2 * halo // 8) * 8
    gap = jnp.zeros(ring.shape[:-1] + (pad - 2 * halo,), ring.dtype)
    block = jnp.concatenate([ring[..., :halo], gap, ring[..., -halo:]], axis=-1)
    return jnp.swapaxes(block, -1, -2)


def sweeps(perturb, adjoint, halo, coef_x, coef_halo, coef_y):
    kl, nf, nl, nr, nq = perturb.shape
    pad = halo.shape[2]
    return pl.pallas_call(
        sweep_kernel,
        grid=(nl,),
        in_specs=[
            pl.BlockSpec((kl, nf, 1, nr, nq), lambda l: (0, 0, l, 0, 0)),
            pl.BlockSpec((nf, 1, nr, nq), lambda l: (0, l, 0, 0)),
            pl.BlockSpec((kl, 1, pad, nr), lambda l: (0, l, 0, 0)),
            pl.BlockSpec((1, nr, nq), lambda l: (l, 0, 0)),
            pl.BlockSpec((1, pad, nr), lambda l: (l, 0, 0)),
            pl.BlockSpec((1, nr, nq), lambda l: (l, 0, 0)),
        ],
        out_specs=pl.BlockSpec((nf, 1, nr, nq), lambda l: (0, l, 0, 0)),
        out_shape=jax.ShapeDtypeStruct((nf, nl, nr, nq), jnp.float32),
    )(perturb, adjoint, halo, coef_x, coef_halo, coef_y)


def on_device(perturb, coef_x, coef_y, obs_values, obs_tile, obs_cell):
    tiles = lax.axis_size("tile")
    mems = lax.axis_size("mem")
    kl, nf, nl, nr, nq = perturb.shape
    members = kl * mems
    halo = SWEEPS
    group = 32
    main = nf * nl * nq
    width = main + 128
    assert tiles >= 3 and tiles & (tiles - 1) == 0 and mems & (mems - 1) == 0
    assert nf * nl * group <= 128 and 2 * halo <= group
    forward = [(i, (i + 1) % tiles) for i in range(tiles)]
    backward = [((i + 1) % tiles, i) for i in range(tiles)]

    widened = perturb.astype(jnp.float32)
    edges = jnp.concatenate([widened.reshape((kl * nf * nl, nr, nq)), coef_x], axis=0)
    from_left = lax.ppermute(edges[..., -halo:], "tile", forward)
    from_right = lax.ppermute(edges[..., :halo], "tile", backward)

    target = obs_tile[:, 0]
    line = obs_cell // nq
    channel = line // nr
    row = line % nr
    column = obs_cell % nq
    dest = jnp.arange(tiles, dtype=jnp.int32)[:, None]
    apart = (target[None, :] - dest) % tiles
    home = channel * nq + column
    lower = main + channel * group + column
    upper = main + channel * group + group - nq + column
    place = jnp.where(apart == 0, home[None, :], jnp.where(apart == 1, lower[None, :], upper[None, :]))
    inside = (apart == 0) | ((apart == 1) & (column[None, :] < halo)) | (
        (apart == tiles - 1) & (column[None, :] >= nq - halo)
    )
    values = jnp.where(inside, obs_values[None, :], 0.0)
    cells = jnp.where(inside, row[None, :] * width + place, 0).astype(jnp.float32)
    outgoing = jnp.stack([values, cells], axis=1)
    me = lax.axis_index("tile")
    own = lax.dynamic_index_in_dim(outgoing, me, 0, keepdims=False)
    field = deposit(own[0], own[1], nr, width)
    for s in range(1, tiles):
        pairs = [(i, i ^ s) for i in range(tiles)]
        sent = lax.dynamic_index_in_dim(outgoing, me ^ s, 0, keepdims=False)
        got = lax.ppermute(sent, "tile", pairs)
        field = field + deposit(got[0], got[1], nr, width)
    field = gather_blocks(scatter_sum(field, "mem", mems), "mem", mems)
    adjoint = jnp.transpose(field[:, :main].reshape(nr, nf, nl, nq), (1, 2, 0, 3))
    rim = jnp.transpose(field[:, main:].reshape(nr, nf, nl, group), (1, 2, 0, 3))

    count = kl * nf * nl
    left_p = from_left[:count].reshape((kl, nf, nl, nr, halo))
    right_p = from_right[:count].reshape((kl, nf, nl, nr, halo))
    left = jnp.sum(left_p * rim[None, ..., group - halo:], axis=1)
    right = jnp.sum(right_p * rim[None, ..., :halo], axis=1)
    pad = -(-2 * halo // 8) * 8
    gap = jnp.zeros(left.shape[:-1] + (pad - 2 * halo,), jnp.float32)
    ring = jnp.swapaxes(jnp.concatenate([right, gap, left], axis=-1), -1, -2)
    cgap = jnp.zeros((nl, nr, pad - 2 * halo), jnp.float32)
    cring = jnp.swapaxes(jnp.concatenate([from_right[count:], cgap, from_left[count:]], axis=-1), -1, -2)
    part = sweeps(perturb, adjoint, ring, coef_x, cring, coef_y)
    blocks = part.reshape((nf, nl, mems, nr // mems, nq))
    blocks = jnp.transpose(blocks, (2, 0, 1, 3, 4))
    summed = jnp.transpose(halving_sum(blocks, "mem", mems), (2, 0, 1, 3))
    return summed / (members - 1)


def solution(mesh):
    return jax.shard_map(
        on_device,
        mesh=mesh,
        in_specs=(
            P("mem", None, None, None, "tile"),
            P(None, None, "tile"),
            P(None, None, "tile"),
            P(("mem", "tile")),
            P(("mem", "tile"), None),
            P(("mem", "tile")),
        ),
        out_specs=P("mem", None, None, "tile"),
        check_vma=False,
    )
```

```python
import jax
import jax.numpy as jnp
from jax import lax
from jax.experimental import pallas as pl
from jax.experimental.pallas import tpu as pltpu
from jax.sharding import PartitionSpec as P

FIELDS = 2
LEVELS = 2
SWEEPS = 6
LAT = 256


def sweep_north(field, coef):
    flux = coef[..., :-1, :] * (field[..., 1:, :] - field[..., :-1, :])
    zero_row = jnp.zeros(field.shape[:-2] + (1, field.shape[-1]), jnp.float32)
    upper = jnp.concatenate([flux, zero_row], axis=-2)
    lower = jnp.concatenate([zero_row, flux], axis=-2)
    return field + upper - lower


def deposit_kernel(hi_ref, lo_ref, row_ref, col_ref, out_ref):
    step = pl.program_id(0)

    @pl.when(step == 0)
    def _():
        out_ref[...] = jnp.zeros(out_ref.shape, jnp.float32)

    rows, width = out_ref.shape
    n = hi_ref.shape[2]
    chunk = 512
    total = jnp.zeros((2 * rows, width), jnp.float32)
    for c0 in range(0, n, chunk):
        sl = slice(c0, c0 + chunk)
        r = row_ref[0, :, sl]
        hit = lax.broadcasted_iota(jnp.int32, (rows, chunk), 0) == r
        zero = jnp.zeros((), jnp.float32)
        a = jnp.concatenate(
            [jnp.where(hit, hi_ref[0, :, sl], zero).astype(jnp.bfloat16),
             jnp.where(hit, lo_ref[0, :, sl], zero).astype(jnp.bfloat16)], axis=0)
        b = (lax.broadcasted_iota(jnp.int32, (width, chunk), 0) == col_ref[0, :, sl]).astype(jnp.bfloat16)
        total = total + lax.dot_general(a, b, (((1,), (1,)), ((), ())), preferred_element_type=jnp.float32)
    out_ref[...] += total[:rows] + total[rows:]


def deposit_all(values, cells, rows, width):
    sources, n = values.shape
    index = cells.astype(jnp.int32)
    row = (index // width)[:, None, :]
    col = (index % width)[:, None, :]
    hi = lax.reduce_precision(values, exponent_bits=8, mantissa_bits=7)
    lo = values - hi
    return pl.pallas_call(
        deposit_kernel,
        grid=(sources,),
        in_specs=[
            pl.BlockSpec((1, 1, n), lambda s: (s, 0, 0)),
            pl.BlockSpec((1, 1, n), lambda s: (s, 0, 0)),
            pl.BlockSpec((1, 1, n), lambda s: (s, 0, 0)),
            pl.BlockSpec((1, 1, n), lambda s: (s, 0, 0)),
        ],
        out_specs=pl.BlockSpec((rows, width), lambda s: (0, 0)),
        out_shape=jax.ShapeDtypeStruct((rows, width), jnp.float32),
    )(hi[:, None, :], lo[:, None, :], row, col)


def exchange(blocks, axis, count):
    me = lax.axis_index(axis)
    out = jnp.zeros_like(blocks)
    out = lax.dynamic_update_index_in_dim(out, lax.dynamic_index_in_dim(blocks, me, 0, keepdims=False), me, 0)
    for s in range(1, count):
        pairs = [(i, i ^ s) for i in range(count)]
        sent = lax.dynamic_index_in_dim(blocks, me ^ s, 0, keepdims=False)
        got = lax.ppermute(sent, axis, pairs)
        out = lax.dynamic_update_index_in_dim(out, got, me ^ s, 0)
    return out


def scatter_sum(x, axis, count):
    blocks = x.reshape((count, x.shape[0] // count) + x.shape[1:])
    return exchange(blocks, axis, count).sum(axis=0)


def gather_blocks(x, axis, count):
    me = lax.axis_index(axis)
    out = jnp.zeros((count,) + x.shape, x.dtype)
    out = lax.dynamic_update_index_in_dim(out, x, me, 0)
    for s in range(1, count):
        pairs = [(i, i ^ s) for i in range(count)]
        out = lax.dynamic_update_index_in_dim(out, lax.ppermute(x, axis, pairs), me ^ s, 0)
    return out.reshape((-1,) + x.shape[1:])


def sweep_kernel(pert_ref, adj_ref, halo_ref, cx_ref, cxh_ref, cy_ref, out_ref):
    kl = pert_ref.shape[0]
    nr, nq = adj_ref.shape[2], adj_ref.shape[3]
    span = nq + halo_ref.shape[2]
    coef = jnp.concatenate([cx_ref[0].T, cxh_ref[0]], axis=0)
    rows = lax.broadcasted_iota(jnp.int32, (nr, nq), 0)
    north = jnp.where(rows < nr - 1, cy_ref[0], 0.0)
    a0 = adj_ref[0, 0]
    a1 = adj_ref[1, 0]
    acc0 = jnp.zeros((nr, nq), jnp.float32)
    acc1 = jnp.zeros((nr, nq), jnp.float32)
    for k in range(kl):
        p0 = pert_ref[k, 0, 0].astype(jnp.float32)
        p1 = pert_ref[k, 1, 0].astype(jnp.float32)
        v = jnp.concatenate([(p0 * a0 + p1 * a1).T, halo_ref[k, 0]], axis=0)
        for step in range(SWEEPS):
            flux = coef * (pltpu.roll(v, span - 1, 0) - v)
            v = v + flux - pltpu.roll(flux, 1, 0)
        v = v[:nq].T
        for step in range(SWEEPS):
            flux = north * (pltpu.roll(v, nr - 1, 0) - v)
            v = v + flux - pltpu.roll(flux, 1, 0)
        acc0 = acc0 + p0 * v
        acc1 = acc1 + p1 * v
    out_ref[0, 0] = acc0
    out_ref[1, 0] = acc1


def turned(ring, halo):
    pad = -(-2 * halo // 8) * 8
    gap = jnp.zeros(ring.shape[:-1] + (pad - 2 * halo,), ring.dtype)
    block = jnp.concatenate([ring[..., :halo], gap, ring[..., -halo:]], axis=-1)
    return jnp.swapaxes(block, -1, -2)


def sweeps(perturb, adjoint, halo, coef_x, coef_halo, coef_y):
    kl, nf, nl, nr, nq = perturb.shape
    pad = halo.shape[2]
    return pl.pallas_call(
        sweep_kernel,
        grid=(nl,),
        in_specs=[
            pl.BlockSpec((kl, nf, 1, nr, nq), lambda l: (0, 0, l, 0, 0)),
            pl.BlockSpec((nf, 1, nr, nq), lambda l: (0, l, 0, 0)),
            pl.BlockSpec((kl, 1, pad, nr), lambda l: (0, l, 0, 0)),
            pl.BlockSpec((1, nr, nq), lambda l: (l, 0, 0)),
            pl.BlockSpec((1, pad, nr), lambda l: (l, 0, 0)),
            pl.BlockSpec((1, nr, nq), lambda l: (l, 0, 0)),
        ],
        out_specs=pl.BlockSpec((nf, 1, nr, nq), lambda l: (0, l, 0, 0)),
        out_shape=jax.ShapeDtypeStruct((nf, nl, nr, nq), jnp.float32),
    )(perturb, adjoint, halo, coef_x, coef_halo, coef_y)


def on_device(perturb, coef_x, coef_y, obs_values, obs_tile, obs_cell):
    tiles = lax.axis_size("tile")
    mems = lax.axis_size("mem")
    kl, nf, nl, nr, nq = perturb.shape
    members = kl * mems
    halo = SWEEPS
    group = 32
    main = nf * nl * nq
    width = main + 128
    assert tiles >= 3 and tiles & (tiles - 1) == 0 and mems & (mems - 1) == 0
    assert nf * nl * group <= 128 and 2 * halo <= group
    forward = [(i, (i + 1) % tiles) for i in range(tiles)]
    backward = [((i + 1) % tiles, i) for i in range(tiles)]

    widened = perturb.astype(jnp.float32)
    edges = jnp.concatenate([widened.reshape((kl * nf * nl, nr, nq)), coef_x], axis=0)
    from_left = lax.ppermute(edges[..., -halo:], "tile", forward)
    from_right = lax.ppermute(edges[..., :halo], "tile", backward)

    target = obs_tile[:, 0]
    line = obs_cell // nq
    channel = line // nr
    row = line % nr
    column = obs_cell % nq
    dest = jnp.arange(tiles, dtype=jnp.int32)[:, None]
    apart = (target[None, :] - dest) % tiles
    home = channel * nq + column
    lower = main + channel * group + column
    upper = main + channel * group + group - nq + column
    place = jnp.where(apart == 0, home[None, :], jnp.where(apart == 1, lower[None, :], upper[None, :]))
    inside = (apart == 0) | ((apart == 1) & (column[None, :] < halo)) | (
        (apart == tiles - 1) & (column[None, :] >= nq - halo)
    )
    values = jnp.where(inside, obs_values[None, :], 0.0)
    cells = jnp.where(inside, row[None, :] * width + place, 0).astype(jnp.float32)
    outgoing = jnp.stack([values, cells], axis=1)
    me = lax.axis_index("tile")
    own = lax.dynamic_index_in_dim(outgoing, me, 0, keepdims=False)
    lists = [own]
    for s in range(1, tiles):
        pairs = [(i, i ^ s) for i in range(tiles)]
        sent = lax.dynamic_index_in_dim(outgoing, me ^ s, 0, keepdims=False)
        lists.append(lax.ppermute(sent, "tile", pairs))
    lists = jnp.stack(lists)
    field = deposit_all(lists[:, 0], lists[:, 1], nr, width)
    field = gather_blocks(scatter_sum(field, "mem", mems), "mem", mems)
    adjoint = jnp.transpose(field[:, :main].reshape(nr, nf, nl, nq), (1, 2, 0, 3))
    rim = jnp.transpose(field[:, main:].reshape(nr, nf, nl, group), (1, 2, 0, 3))

    count = kl * nf * nl
    left_p = from_left[:count].reshape((kl, nf, nl, nr, halo))
    right_p = from_right[:count].reshape((kl, nf, nl, nr, halo))
    left = jnp.sum(left_p * rim[None, ..., group - halo:], axis=1)
    right = jnp.sum(right_p * rim[None, ..., :halo], axis=1)
    pad = -(-2 * halo // 8) * 8
    gap = jnp.zeros(left.shape[:-1] + (pad - 2 * halo,), jnp.float32)
    ring = jnp.swapaxes(jnp.concatenate([right, gap, left], axis=-1), -1, -2)
    cgap = jnp.zeros((nl, nr, pad - 2 * halo), jnp.float32)
    cring = jnp.swapaxes(jnp.concatenate([from_right[count:], cgap, from_left[count:]], axis=-1), -1, -2)
    part = sweeps(perturb, adjoint, ring, coef_x, cring, coef_y)
    blocks = part.reshape((nf, nl, mems, nr // mems, nq))
    blocks = jnp.transpose(blocks, (2, 0, 1, 3, 4))
    summed = jnp.transpose(exchange(blocks, "mem", mems).sum(axis=0), (2, 0, 1, 3))
    return summed / (members - 1)


def solution(mesh):
    return jax.shard_map(
        on_device,
        mesh=mesh,
        in_specs=(
            P("mem", None, None, None, "tile"),
            P(None, None, "tile"),
            P(None, None, "tile"),
            P(("mem", "tile")),
            P(("mem", "tile"), None),
            P(("mem", "tile")),
        ),
        out_specs=P("mem", None, None, "tile"),
        check_vma=False,
    )
```

```python
import jax
import jax.numpy as jnp
from jax import lax
from jax.experimental import pallas as pl
from jax.experimental.pallas import tpu as pltpu
from jax.sharding import PartitionSpec as P

FIELDS = 2
LEVELS = 2
SWEEPS = 6
LAT = 256


def sweep_north(field, coef):
    flux = coef[..., :-1, :] * (field[..., 1:, :] - field[..., :-1, :])
    zero_row = jnp.zeros(field.shape[:-2] + (1, field.shape[-1]), jnp.float32)
    upper = jnp.concatenate([flux, zero_row], axis=-2)
    lower = jnp.concatenate([zero_row, flux], axis=-2)
    return field + upper - lower


def deposit_kernel(hi_ref, lo_ref, row_ref, col_ref, out_ref):
    step = pl.program_id(0)

    @pl.when(step == 0)
    def _():
        out_ref[...] = jnp.zeros(out_ref.shape, jnp.float32)

    rows, width = out_ref.shape
    n = hi_ref.shape[2]
    chunk = 512
    total = jnp.zeros((2 * rows, width), jnp.float32)
    for c0 in range(0, n, chunk):
        sl = slice(c0, c0 + chunk)
        r = row_ref[0, :, sl]
        hit = lax.broadcasted_iota(jnp.int32, (rows, chunk), 0) == r
        zero = jnp.zeros((), jnp.float32)
        a = jnp.concatenate(
            [jnp.where(hit, hi_ref[0, :, sl], zero).astype(jnp.bfloat16),
             jnp.where(hit, lo_ref[0, :, sl], zero).astype(jnp.bfloat16)], axis=0)
        b = (lax.broadcasted_iota(jnp.int32, (width, chunk), 0) == col_ref[0, :, sl]).astype(jnp.bfloat16)
        total = total + lax.dot_general(a, b, (((1,), (1,)), ((), ())), preferred_element_type=jnp.float32)
    out_ref[...] += total[:rows] + total[rows:]


def deposit_all(values, cells, rows, width):
    sources, n = values.shape
    index = cells.astype(jnp.int32)
    row = (index // width)[:, None, :]
    col = (index % width)[:, None, :]
    hi = lax.reduce_precision(values, exponent_bits=8, mantissa_bits=7)
    lo = values - hi
    return pl.pallas_call(
        deposit_kernel,
        grid=(sources,),
        in_specs=[
            pl.BlockSpec((1, 1, n), lambda s: (s, 0, 0)),
            pl.BlockSpec((1, 1, n), lambda s: (s, 0, 0)),
            pl.BlockSpec((1, 1, n), lambda s: (s, 0, 0)),
            pl.BlockSpec((1, 1, n), lambda s: (s, 0, 0)),
        ],
        out_specs=pl.BlockSpec((rows, width), lambda s: (0, 0)),
        out_shape=jax.ShapeDtypeStruct((rows, width), jnp.float32),
    )(hi[:, None, :], lo[:, None, :], row, col)


def exchange(blocks, axis, count):
    me = lax.axis_index(axis)
    out = jnp.zeros_like(blocks)
    out = lax.dynamic_update_index_in_dim(out, lax.dynamic_index_in_dim(blocks, me, 0, keepdims=False), me, 0)
    for s in range(1, count):
        pairs = [(i, i ^ s) for i in range(count)]
        sent = lax.dynamic_index_in_dim(blocks, me ^ s, 0, keepdims=False)
        got = lax.ppermute(sent, axis, pairs)
        out = lax.dynamic_update_index_in_dim(out, got, me ^ s, 0)
    return out


def scatter_sum(x, axis, count):
    blocks = x.reshape((count, x.shape[0] // count) + x.shape[1:])
    return exchange(blocks, axis, count).sum(axis=0)


def gather_blocks(x, axis, count):
    me = lax.axis_index(axis)
    out = jnp.zeros((count,) + x.shape, x.dtype)
    out = lax.dynamic_update_index_in_dim(out, x, me, 0)
    for s in range(1, count):
        pairs = [(i, i ^ s) for i in range(count)]
        out = lax.dynamic_update_index_in_dim(out, lax.ppermute(x, axis, pairs), me ^ s, 0)
    return out.reshape((-1,) + x.shape[1:])


def sweep_kernel(pert_ref, adj_ref, halo_ref, cx_ref, cxh_ref, cy_ref, out_ref):
    kl = pert_ref.shape[0]
    nr, nq = adj_ref.shape[2], adj_ref.shape[3]
    span = nq + halo_ref.shape[2]
    coef = jnp.concatenate([cx_ref[0].T, cxh_ref[0]], axis=0)
    rows = lax.broadcasted_iota(jnp.int32, (nr, nq), 0)
    north = jnp.where(rows < nr - 1, cy_ref[0], 0.0)
    a0 = adj_ref[0, 0]
    a1 = adj_ref[1, 0]
    acc0 = jnp.zeros((nr, nq), jnp.float32)
    acc1 = jnp.zeros((nr, nq), jnp.float32)
    for k in range(kl):
        p0 = pert_ref[k, 0, 0].astype(jnp.float32)
        p1 = pert_ref[k, 1, 0].astype(jnp.float32)
        v = jnp.concatenate([(p0 * a0 + p1 * a1).T, halo_ref[k, 0]], axis=0)
        for step in range(SWEEPS):
            flux = coef * (pltpu.roll(v, span - 1, 0) - v)
            v = v + flux - pltpu.roll(flux, 1, 0)
        v = v[:nq].T
        for step in range(SWEEPS):
            flux = north * (pltpu.roll(v, nr - 1, 0) - v)
            v = v + flux - pltpu.roll(flux, 1, 0)
        acc0 = acc0 + p0 * v
        acc1 = acc1 + p1 * v
    out_ref[0, 0] = acc0
    out_ref[1, 0] = acc1


def turned(ring, halo):
    pad = -(-2 * halo // 8) * 8
    gap = jnp.zeros(ring.shape[:-1] + (pad - 2 * halo,), ring.dtype)
    block = jnp.concatenate([ring[..., :halo], gap, ring[..., -halo:]], axis=-1)
    return jnp.swapaxes(block, -1, -2)


def sweeps(perturb, adjoint, halo, coef_x, coef_halo, coef_y):
    kl, nf, nl, nr, nq = perturb.shape
    pad = halo.shape[2]
    return pl.pallas_call(
        sweep_kernel,
        grid=(nl,),
        in_specs=[
            pl.BlockSpec((kl, nf, 1, nr, nq), lambda l: (0, 0, l, 0, 0)),
            pl.BlockSpec((nf, 1, nr, nq), lambda l: (0, l, 0, 0)),
            pl.BlockSpec((kl, 1, pad, nr), lambda l: (0, l, 0, 0)),
            pl.BlockSpec((1, nr, nq), lambda l: (l, 0, 0)),
            pl.BlockSpec((1, pad, nr), lambda l: (l, 0, 0)),
            pl.BlockSpec((1, nr, nq), lambda l: (l, 0, 0)),
        ],
        out_specs=pl.BlockSpec((nf, 1, nr, nq), lambda l: (0, l, 0, 0)),
        out_shape=jax.ShapeDtypeStruct((nf, nl, nr, nq), jnp.float32),
    )(perturb, adjoint, halo, coef_x, coef_halo, coef_y)


def on_device(perturb, coef_x, coef_y, obs_values, obs_tile, obs_cell):
    tiles = lax.axis_size("tile")
    mems = lax.axis_size("mem")
    kl, nf, nl, nr, nq = perturb.shape
    members = kl * mems
    halo = SWEEPS
    group = 32
    main = nf * nl * nq
    width = main + 128
    assert tiles >= 3 and tiles & (tiles - 1) == 0 and mems & (mems - 1) == 0
    assert nf * nl * group <= 128 and 2 * halo <= group
    forward = [(i, (i + 1) % tiles) for i in range(tiles)]
    backward = [((i + 1) % tiles, i) for i in range(tiles)]

    widened = perturb.astype(jnp.float32)
    flat = perturb.reshape((kl * nf * nl, nr, nq))
    high = jnp.concatenate([flat[..., -halo:].astype(jnp.float32), coef_x[..., -halo:]], axis=0)
    low = jnp.concatenate([flat[..., :halo].astype(jnp.float32), coef_x[..., :halo]], axis=0)
    from_left = lax.ppermute(high, "tile", forward)
    from_right = lax.ppermute(low, "tile", backward)

    target = obs_tile[:, 0]
    line = obs_cell // nq
    channel = line // nr
    row = line % nr
    column = obs_cell % nq
    dest = jnp.arange(tiles, dtype=jnp.int32)[:, None]
    apart = (target[None, :] - dest) % tiles
    home = channel * nq + column
    lower = main + channel * group + column
    upper = main + channel * group + group - nq + column
    place = jnp.where(apart == 0, home[None, :], jnp.where(apart == 1, lower[None, :], upper[None, :]))
    inside = (apart == 0) | ((apart == 1) & (column[None, :] < halo)) | (
        (apart == tiles - 1) & (column[None, :] >= nq - halo)
    )
    values = jnp.where(inside, obs_values[None, :], 0.0)
    cells = jnp.where(inside, row[None, :] * width + place, 0).astype(jnp.float32)
    outgoing = jnp.stack([values, cells], axis=1)
    me = lax.axis_index("tile")
    own = lax.dynamic_index_in_dim(outgoing, me, 0, keepdims=False)
    lists = [own]
    for s in range(1, tiles):
        pairs = [(i, i ^ s) for i in range(tiles)]
        sent = lax.dynamic_index_in_dim(outgoing, me ^ s, 0, keepdims=False)
        lists.append(lax.ppermute(sent, "tile", pairs))
    lists = jnp.stack(lists)
    field = deposit_all(lists[:, 0], lists[:, 1], nr, width)
    field = gather_blocks(scatter_sum(field, "mem", mems), "mem", mems)
    adjoint = jnp.transpose(field[:, :main].reshape(nr, nf, nl, nq), (1, 2, 0, 3))
    rim = jnp.transpose(field[:, main:].reshape(nr, nf, nl, group), (1, 2, 0, 3))

    count = kl * nf * nl
    left_p = from_left[:count].reshape((kl, nf, nl, nr, halo))
    right_p = from_right[:count].reshape((kl, nf, nl, nr, halo))
    left = jnp.sum(left_p * rim[None, ..., group - halo:], axis=1)
    right = jnp.sum(right_p * rim[None, ..., :halo], axis=1)
    pad = -(-2 * halo // 8) * 8
    gap = jnp.zeros(left.shape[:-1] + (pad - 2 * halo,), jnp.float32)
    ring = jnp.swapaxes(jnp.concatenate([right, gap, left], axis=-1), -1, -2)
    cgap = jnp.zeros((nl, nr, pad - 2 * halo), jnp.float32)
    cring = jnp.swapaxes(jnp.concatenate([from_right[count:], cgap, from_left[count:]], axis=-1), -1, -2)
    part = sweeps(perturb, adjoint, ring, coef_x, cring, coef_y)
    blocks = part.reshape((nf, nl, mems, nr // mems, nq))
    blocks = jnp.transpose(blocks, (2, 0, 1, 3, 4))
    summed = jnp.transpose(exchange(blocks, "mem", mems).sum(axis=0), (2, 0, 1, 3))
    return summed / (members - 1)


def solution(mesh):
    return jax.shard_map(
        on_device,
        mesh=mesh,
        in_specs=(
            P("mem", None, None, None, "tile"),
            P(None, None, "tile"),
            P(None, None, "tile"),
            P(("mem", "tile")),
            P(("mem", "tile"), None),
            P(("mem", "tile")),
        ),
        out_specs=P("mem", None, None, "tile"),
        check_vma=False,
    )
```

```python
import jax
import jax.numpy as jnp
from jax import lax
from jax.experimental import pallas as pl
from jax.experimental.pallas import tpu as pltpu
from jax.sharding import PartitionSpec as P

FIELDS = 2
LEVELS = 2
SWEEPS = 6
LAT = 256


def sweep_north(field, coef):
    flux = coef[..., :-1, :] * (field[..., 1:, :] - field[..., :-1, :])
    zero_row = jnp.zeros(field.shape[:-2] + (1, field.shape[-1]), jnp.float32)
    upper = jnp.concatenate([flux, zero_row], axis=-2)
    lower = jnp.concatenate([zero_row, flux], axis=-2)
    return field + upper - lower


def deposit_kernel(hi_ref, lo_ref, row_ref, col_ref, out_ref):
    step = pl.program_id(0)

    @pl.when(step == 0)
    def _():
        out_ref[...] = jnp.zeros(out_ref.shape, jnp.float32)

    rows, width = out_ref.shape
    n = hi_ref.shape[2]
    chunk = 512
    total = jnp.zeros((2 * rows, width), jnp.float32)
    for c0 in range(0, n, chunk):
        sl = slice(c0, c0 + chunk)
        r = row_ref[0, :, sl]
        hit = lax.broadcasted_iota(jnp.int32, (rows, chunk), 0) == r
        zero = jnp.zeros((), jnp.float32)
        a = jnp.concatenate(
            [jnp.where(hit, hi_ref[0, :, sl], zero).astype(jnp.bfloat16),
             jnp.where(hit, lo_ref[0, :, sl], zero).astype(jnp.bfloat16)], axis=0)
        b = (lax.broadcasted_iota(jnp.int32, (width, chunk), 0) == col_ref[0, :, sl]).astype(jnp.bfloat16)
        total = total + lax.dot_general(a, b, (((1,), (1,)), ((), ())), preferred_element_type=jnp.float32)
    out_ref[...] += total[:rows] + total[rows:]


def deposit_all(values, cells, rows, width):
    sources, n = values.shape
    index = cells.astype(jnp.int32)
    row = (index // width)[:, None, :]
    col = (index % width)[:, None, :]
    hi = lax.reduce_precision(values, exponent_bits=8, mantissa_bits=7)
    lo = values - hi
    return pl.pallas_call(
        deposit_kernel,
        grid=(sources,),
        in_specs=[
            pl.BlockSpec((1, 1, n), lambda s: (s, 0, 0)),
            pl.BlockSpec((1, 1, n), lambda s: (s, 0, 0)),
            pl.BlockSpec((1, 1, n), lambda s: (s, 0, 0)),
            pl.BlockSpec((1, 1, n), lambda s: (s, 0, 0)),
        ],
        out_specs=pl.BlockSpec((rows, width), lambda s: (0, 0)),
        out_shape=jax.ShapeDtypeStruct((rows, width), jnp.float32),
    )(hi[:, None, :], lo[:, None, :], row, col)


def exchange(blocks, axis, count):
    me = lax.axis_index(axis)
    out = jnp.zeros_like(blocks)
    out = lax.dynamic_update_index_in_dim(out, lax.dynamic_index_in_dim(blocks, me, 0, keepdims=False), me, 0)
    for s in range(1, count):
        pairs = [(i, i ^ s) for i in range(count)]
        sent = lax.dynamic_index_in_dim(blocks, me ^ s, 0, keepdims=False)
        got = lax.ppermute(sent, axis, pairs)
        out = lax.dynamic_update_index_in_dim(out, got, me ^ s, 0)
    return out


def scatter_sum(x, axis, count):
    blocks = x.reshape((count, x.shape[0] // count) + x.shape[1:])
    return exchange(blocks, axis, count).sum(axis=0)


def gather_blocks(x, axis, count):
    me = lax.axis_index(axis)
    out = jnp.zeros((count,) + x.shape, x.dtype)
    out = lax.dynamic_update_index_in_dim(out, x, me, 0)
    for s in range(1, count):
        pairs = [(i, i ^ s) for i in range(count)]
        out = lax.dynamic_update_index_in_dim(out, lax.ppermute(x, axis, pairs), me ^ s, 0)
    return out.reshape((-1,) + x.shape[1:])


def sweep_kernel(pert_ref, a0_ref, a1_ref, halo_ref, cx_ref, cxh_ref, cy_ref, out_ref):
    kl = pert_ref.shape[0]
    nr, nq = a0_ref.shape
    span = nq + halo_ref.shape[2]
    coef = jnp.concatenate([cx_ref[0].T, cxh_ref[0]], axis=0)
    rows = lax.broadcasted_iota(jnp.int32, (nr, nq), 0)
    north = jnp.where(rows < nr - 1, cy_ref[0], 0.0)
    a0 = a0_ref[...]
    a1 = a1_ref[...]
    acc0 = jnp.zeros((nr, nq), jnp.float32)
    acc1 = jnp.zeros((nr, nq), jnp.float32)
    for k in range(kl):
        p0 = pert_ref[k, 0, 0].astype(jnp.float32)
        p1 = pert_ref[k, 1, 0].astype(jnp.float32)
        v = jnp.concatenate([(p0 * a0 + p1 * a1).T, halo_ref[k, 0]], axis=0)
        for step in range(SWEEPS):
            flux = coef * (pltpu.roll(v, span - 1, 0) - v)
            v = v + flux - pltpu.roll(flux, 1, 0)
        v = v[:nq].T
        for step in range(SWEEPS):
            flux = north * (pltpu.roll(v, nr - 1, 0) - v)
            v = v + flux - pltpu.roll(flux, 1, 0)
        acc0 = acc0 + p0 * v
        acc1 = acc1 + p1 * v
    out_ref[0, 0] = acc0
    out_ref[1, 0] = acc1


def turned(ring, halo):
    pad = -(-2 * halo // 8) * 8
    gap = jnp.zeros(ring.shape[:-1] + (pad - 2 * halo,), ring.dtype)
    block = jnp.concatenate([ring[..., :halo], gap, ring[..., -halo:]], axis=-1)
    return jnp.swapaxes(block, -1, -2)


def sweeps(perturb, field, halo, coef_x, coef_halo, coef_y):
    kl, nf, nl, nr, nq = perturb.shape
    assert nf == 2
    pad = halo.shape[2]
    return pl.pallas_call(
        sweep_kernel,
        grid=(nl,),
        in_specs=[
            pl.BlockSpec((kl, nf, 1, nr, nq), lambda l: (0, 0, l, 0, 0)),
            pl.BlockSpec((nr, nq), lambda l: (0, l)),
            pl.BlockSpec((nr, nq), lambda l: (0, nl + l)),
            pl.BlockSpec((kl, 1, pad, nr), lambda l: (0, l, 0, 0)),
            pl.BlockSpec((1, nr, nq), lambda l: (l, 0, 0)),
            pl.BlockSpec((1, pad, nr), lambda l: (l, 0, 0)),
            pl.BlockSpec((1, nr, nq), lambda l: (l, 0, 0)),
        ],
        out_specs=pl.BlockSpec((nf, 1, nr, nq), lambda l: (0, l, 0, 0)),
        out_shape=jax.ShapeDtypeStruct((nf, nl, nr, nq), jnp.float32),
    )(perturb, field, field, halo, coef_x, coef_halo, coef_y)


def on_device(perturb, coef_x, coef_y, obs_values, obs_tile, obs_cell):
    tiles = lax.axis_size("tile")
    mems = lax.axis_size("mem")
    kl, nf, nl, nr, nq = perturb.shape
    members = kl * mems
    halo = SWEEPS
    group = 32
    main = nf * nl * nq
    width = main + 128
    assert tiles >= 3 and tiles & (tiles - 1) == 0 and mems & (mems - 1) == 0
    assert nf * nl * group <= 128 and 2 * halo <= group
    forward = [(i, (i + 1) % tiles) for i in range(tiles)]
    backward = [((i + 1) % tiles, i) for i in range(tiles)]

    widened = perturb.astype(jnp.float32)
    flat = perturb.reshape((kl * nf * nl, nr, nq))
    high = jnp.concatenate([flat[..., -halo:].astype(jnp.float32), coef_x[..., -halo:]], axis=0)
    low = jnp.concatenate([flat[..., :halo].astype(jnp.float32), coef_x[..., :halo]], axis=0)
    from_left = lax.ppermute(high, "tile", forward)
    from_right = lax.ppermute(low, "tile", backward)

    target = obs_tile[:, 0]
    line = obs_cell // nq
    channel = line // nr
    row = line % nr
    column = obs_cell % nq
    dest = jnp.arange(tiles, dtype=jnp.int32)[:, None]
    apart = (target[None, :] - dest) % tiles
    home = channel * nq + column
    lower = main + channel * group + column
    upper = main + channel * group + group - nq + column
    place = jnp.where(apart == 0, home[None, :], jnp.where(apart == 1, lower[None, :], upper[None, :]))
    inside = (apart == 0) | ((apart == 1) & (column[None, :] < halo)) | (
        (apart == tiles - 1) & (column[None, :] >= nq - halo)
    )
    values = jnp.where(inside, obs_values[None, :], 0.0)
    cells = jnp.where(inside, row[None, :] * width + place, 0).astype(jnp.float32)
    outgoing = jnp.stack([values, cells], axis=1)
    me = lax.axis_index("tile")
    own = lax.dynamic_index_in_dim(outgoing, me, 0, keepdims=False)
    lists = [own]
    for s in range(1, tiles):
        pairs = [(i, i ^ s) for i in range(tiles)]
        sent = lax.dynamic_index_in_dim(outgoing, me ^ s, 0, keepdims=False)
        lists.append(lax.ppermute(sent, "tile", pairs))
    lists = jnp.stack(lists)
    field = deposit_all(lists[:, 0], lists[:, 1], nr, width)
    field = gather_blocks(scatter_sum(field, "mem", mems), "mem", mems)
    rim = jnp.transpose(field[:, main:].reshape(nr, nf, nl, group), (1, 2, 0, 3))

    count = kl * nf * nl
    left_p = from_left[:count].reshape((kl, nf, nl, nr, halo))
    right_p = from_right[:count].reshape((kl, nf, nl, nr, halo))
    left = jnp.sum(left_p * rim[None, ..., group - halo:], axis=1)
    right = jnp.sum(right_p * rim[None, ..., :halo], axis=1)
    pad = -(-2 * halo // 8) * 8
    gap = jnp.zeros(left.shape[:-1] + (pad - 2 * halo,), jnp.float32)
    ring = jnp.swapaxes(jnp.concatenate([right, gap, left], axis=-1), -1, -2)
    cgap = jnp.zeros((nl, nr, pad - 2 * halo), jnp.float32)
    cring = jnp.swapaxes(jnp.concatenate([from_right[count:], cgap, from_left[count:]], axis=-1), -1, -2)
    part = sweeps(perturb, field, ring, coef_x, cring, coef_y)
    blocks = part.reshape((nf, nl, mems, nr // mems, nq))
    blocks = jnp.transpose(blocks, (2, 0, 1, 3, 4))
    summed = jnp.transpose(exchange(blocks, "mem", mems).sum(axis=0), (2, 0, 1, 3))
    return summed / (members - 1)


def solution(mesh):
    return jax.shard_map(
        on_device,
        mesh=mesh,
        in_specs=(
            P("mem", None, None, None, "tile"),
            P(None, None, "tile"),
            P(None, None, "tile"),
            P(("mem", "tile")),
            P(("mem", "tile"), None),
            P(("mem", "tile")),
        ),
        out_specs=P("mem", None, None, "tile"),
        check_vma=False,
    )
```

```python
import jax
import jax.numpy as jnp
from jax import lax
from jax.experimental import pallas as pl
from jax.experimental.pallas import tpu as pltpu
from jax.sharding import PartitionSpec as P

FIELDS = 2
LEVELS = 2
SWEEPS = 6
LAT = 256


def sweep_north(field, coef):
    flux = coef[..., :-1, :] * (field[..., 1:, :] - field[..., :-1, :])
    zero_row = jnp.zeros(field.shape[:-2] + (1, field.shape[-1]), jnp.float32)
    upper = jnp.concatenate([flux, zero_row], axis=-2)
    lower = jnp.concatenate([zero_row, flux], axis=-2)
    return field + upper - lower


def deposit_kernel(hi_ref, lo_ref, row_ref, col_ref, out_ref):
    step = pl.program_id(0)

    @pl.when(step == 0)
    def _():
        out_ref[...] = jnp.zeros(out_ref.shape, jnp.float32)

    rows, width = out_ref.shape
    n = hi_ref.shape[2]
    chunk = 512
    total = jnp.zeros((2 * rows, width), jnp.float32)
    for c0 in range(0, n, chunk):
        sl = slice(c0, c0 + chunk)
        r = row_ref[0, :, sl]
        hit = lax.broadcasted_iota(jnp.int32, (rows, chunk), 0) == r
        zero = jnp.zeros((), jnp.float32)
        a = jnp.concatenate(
            [jnp.where(hit, hi_ref[0, :, sl], zero).astype(jnp.bfloat16),
             jnp.where(hit, lo_ref[0, :, sl], zero).astype(jnp.bfloat16)], axis=0)
        b = (lax.broadcasted_iota(jnp.int32, (width, chunk), 0) == col_ref[0, :, sl]).astype(jnp.bfloat16)
        total = total + lax.dot_general(a, b, (((1,), (1,)), ((), ())), preferred_element_type=jnp.float32)
    out_ref[...] += total[:rows] + total[rows:]


def deposit_all(values, cells, rows, width):
    sources, n = values.shape
    index = cells.astype(jnp.int32)
    row = (index // width)[:, None, :]
    col = (index % width)[:, None, :]
    hi = lax.reduce_precision(values, exponent_bits=8, mantissa_bits=7)
    lo = values - hi
    return pl.pallas_call(
        deposit_kernel,
        grid=(sources,),
        in_specs=[
            pl.BlockSpec((1, 1, n), lambda s: (s, 0, 0)),
            pl.BlockSpec((1, 1, n), lambda s: (s, 0, 0)),
            pl.BlockSpec((1, 1, n), lambda s: (s, 0, 0)),
            pl.BlockSpec((1, 1, n), lambda s: (s, 0, 0)),
        ],
        out_specs=pl.BlockSpec((rows, width), lambda s: (0, 0)),
        out_shape=jax.ShapeDtypeStruct((rows, width), jnp.float32),
    )(hi[:, None, :], lo[:, None, :], row, col)


def exchange(blocks, axis, count):
    me = lax.axis_index(axis)
    out = jnp.zeros_like(blocks)
    out = lax.dynamic_update_index_in_dim(out, lax.dynamic_index_in_dim(blocks, me, 0, keepdims=False), me, 0)
    for s in range(1, count):
        pairs = [(i, i ^ s) for i in range(count)]
        sent = lax.dynamic_index_in_dim(blocks, me ^ s, 0, keepdims=False)
        got = lax.ppermute(sent, axis, pairs)
        out = lax.dynamic_update_index_in_dim(out, got, me ^ s, 0)
    return out


def scatter_sum(x, axis, count):
    blocks = x.reshape((count, x.shape[0] // count) + x.shape[1:])
    return exchange(blocks, axis, count).sum(axis=0)


def gather_blocks(x, axis, count):
    me = lax.axis_index(axis)
    out = jnp.zeros((count,) + x.shape, x.dtype)
    out = lax.dynamic_update_index_in_dim(out, x, me, 0)
    for s in range(1, count):
        pairs = [(i, i ^ s) for i in range(count)]
        out = lax.dynamic_update_index_in_dim(out, lax.ppermute(x, axis, pairs), me ^ s, 0)
    return out.reshape((-1,) + x.shape[1:])


def sweep_kernel(pert_ref, a0_ref, a1_ref, halo_ref, cx_ref, cxh_ref, cy_ref, out_ref):
    kl = pert_ref.shape[0]
    nr, nq = a0_ref.shape
    span = nq + halo_ref.shape[2]
    coef = jnp.concatenate([cx_ref[0].T, cxh_ref[0]], axis=0)
    rows = lax.broadcasted_iota(jnp.int32, (nr, nq), 0)
    north = jnp.where(rows < nr - 1, cy_ref[0], 0.0)
    a0 = a0_ref[...]
    a1 = a1_ref[...]
    acc0 = jnp.zeros((nr, nq), jnp.float32)
    acc1 = jnp.zeros((nr, nq), jnp.float32)
    for k in range(kl):
        p0 = pert_ref[k, 0, 0].astype(jnp.float32)
        p1 = pert_ref[k, 1, 0].astype(jnp.float32)
        v = jnp.concatenate([(p0 * a0 + p1 * a1).T, halo_ref[k, 0]], axis=0)
        for step in range(SWEEPS):
            flux = coef * (pltpu.roll(v, span - 1, 0) - v)
            v = v + flux - pltpu.roll(flux, 1, 0)
        v = v[:nq].T
        for step in range(SWEEPS):
            flux = north * (pltpu.roll(v, nr - 1, 0) - v)
            v = v + flux - pltpu.roll(flux, 1, 0)
        acc0 = acc0 + p0 * v
        acc1 = acc1 + p1 * v
    parts = out_ref.shape[0]
    out_ref[:, 0, 0] = acc0.reshape(parts, nr // parts, nq)
    out_ref[:, 1, 0] = acc1.reshape(parts, nr // parts, nq)


def turned(ring, halo):
    pad = -(-2 * halo // 8) * 8
    gap = jnp.zeros(ring.shape[:-1] + (pad - 2 * halo,), ring.dtype)
    block = jnp.concatenate([ring[..., :halo], gap, ring[..., -halo:]], axis=-1)
    return jnp.swapaxes(block, -1, -2)


def sweeps(perturb, field, halo, coef_x, coef_halo, coef_y, parts):
    kl, nf, nl, nr, nq = perturb.shape
    assert nf == 2
    pad = halo.shape[2]
    return pl.pallas_call(
        sweep_kernel,
        grid=(nl,),
        in_specs=[
            pl.BlockSpec((kl, nf, 1, nr, nq), lambda l: (0, 0, l, 0, 0)),
            pl.BlockSpec((nr, nq), lambda l: (0, l)),
            pl.BlockSpec((nr, nq), lambda l: (0, nl + l)),
            pl.BlockSpec((kl, 1, pad, nr), lambda l: (0, l, 0, 0)),
            pl.BlockSpec((1, nr, nq), lambda l: (l, 0, 0)),
            pl.BlockSpec((1, pad, nr), lambda l: (l, 0, 0)),
            pl.BlockSpec((1, nr, nq), lambda l: (l, 0, 0)),
        ],
        out_specs=pl.BlockSpec((parts, nf, 1, nr // parts, nq), lambda l: (0, 0, l, 0, 0)),
        out_shape=jax.ShapeDtypeStruct((parts, nf, nl, nr // parts, nq), jnp.float32),
    )(perturb, field, field, halo, coef_x, coef_halo, coef_y)


def on_device(perturb, coef_x, coef_y, obs_values, obs_tile, obs_cell):
    tiles = lax.axis_size("tile")
    mems = lax.axis_size("mem")
    kl, nf, nl, nr, nq = perturb.shape
    members = kl * mems
    halo = SWEEPS
    group = 32
    main = nf * nl * nq
    width = main + 128
    assert tiles >= 3 and tiles & (tiles - 1) == 0 and mems & (mems - 1) == 0
    assert nf * nl * group <= 128 and 2 * halo <= group
    forward = [(i, (i + 1) % tiles) for i in range(tiles)]
    backward = [((i + 1) % tiles, i) for i in range(tiles)]

    widened = perturb.astype(jnp.float32)
    flat = perturb.reshape((kl * nf * nl, nr, nq))
    high = jnp.concatenate([flat[..., -halo:].astype(jnp.float32), coef_x[..., -halo:]], axis=0)
    low = jnp.concatenate([flat[..., :halo].astype(jnp.float32), coef_x[..., :halo]], axis=0)
    from_left = lax.ppermute(high, "tile", forward)
    from_right = lax.ppermute(low, "tile", backward)

    target = obs_tile[:, 0]
    line = obs_cell // nq
    channel = line // nr
    row = line % nr
    column = obs_cell % nq
    dest = jnp.arange(tiles, dtype=jnp.int32)[:, None]
    apart = (target[None, :] - dest) % tiles
    home = channel * nq + column
    lower = main + channel * group + column
    upper = main + channel * group + group - nq + column
    place = jnp.where(apart == 0, home[None, :], jnp.where(apart == 1, lower[None, :], upper[None, :]))
    inside = (apart == 0) | ((apart == 1) & (column[None, :] < halo)) | (
        (apart == tiles - 1) & (column[None, :] >= nq - halo)
    )
    values = jnp.where(inside, obs_values[None, :], 0.0)
    cells = jnp.where(inside, row[None, :] * width + place, 0).astype(jnp.float32)
    outgoing = jnp.stack([values, cells], axis=1)
    me = lax.axis_index("tile")
    own = lax.dynamic_index_in_dim(outgoing, me, 0, keepdims=False)
    lists = [own]
    for s in range(1, tiles):
        pairs = [(i, i ^ s) for i in range(tiles)]
        sent = lax.dynamic_index_in_dim(outgoing, me ^ s, 0, keepdims=False)
        lists.append(lax.ppermute(sent, "tile", pairs))
    lists = jnp.stack(lists)
    field = deposit_all(lists[:, 0], lists[:, 1], nr, width)
    field = gather_blocks(scatter_sum(field, "mem", mems), "mem", mems)
    rim = jnp.transpose(field[:, main:].reshape(nr, nf, nl, group), (1, 2, 0, 3))

    count = kl * nf * nl
    left_p = from_left[:count].reshape((kl, nf, nl, nr, halo))
    right_p = from_right[:count].reshape((kl, nf, nl, nr, halo))
    left = jnp.sum(left_p * rim[None, ..., group - halo:], axis=1)
    right = jnp.sum(right_p * rim[None, ..., :halo], axis=1)
    pad = -(-2 * halo // 8) * 8
    gap = jnp.zeros(left.shape[:-1] + (pad - 2 * halo,), jnp.float32)
    ring = jnp.swapaxes(jnp.concatenate([right, gap, left], axis=-1), -1, -2)
    cgap = jnp.zeros((nl, nr, pad - 2 * halo), jnp.float32)
    cring = jnp.swapaxes(jnp.concatenate([from_right[count:], cgap, from_left[count:]], axis=-1), -1, -2)
    blocks = sweeps(perturb, field, ring, coef_x, cring, coef_y, mems)
    summed = jnp.transpose(exchange(blocks, "mem", mems).sum(axis=0), (2, 0, 1, 3))
    return summed / (members - 1)


def solution(mesh):
    return jax.shard_map(
        on_device,
        mesh=mesh,
        in_specs=(
            P("mem", None, None, None, "tile"),
            P(None, None, "tile"),
            P(None, None, "tile"),
            P(("mem", "tile")),
            P(("mem", "tile"), None),
            P(("mem", "tile")),
        ),
        out_specs=P("mem", None, None, "tile"),
        check_vma=False,
    )
```

```python
import jax
import jax.numpy as jnp
from jax import lax
from jax.experimental import pallas as pl
from jax.experimental.pallas import tpu as pltpu
from jax.sharding import PartitionSpec as P

FIELDS = 2
LEVELS = 2
SWEEPS = 6
LAT = 256


def sweep_north(field, coef):
    flux = coef[..., :-1, :] * (field[..., 1:, :] - field[..., :-1, :])
    zero_row = jnp.zeros(field.shape[:-2] + (1, field.shape[-1]), jnp.float32)
    upper = jnp.concatenate([flux, zero_row], axis=-2)
    lower = jnp.concatenate([zero_row, flux], axis=-2)
    return field + upper - lower


def deposit_kernel(hi_ref, lo_ref, row_ref, col_ref, out_ref):
    step = pl.program_id(0)

    @pl.when(step == 0)
    def _():
        out_ref[...] = jnp.zeros(out_ref.shape, jnp.float32)

    rows, width = out_ref.shape
    n = hi_ref.shape[2]
    chunk = 512
    total = jnp.zeros((2 * rows, width), jnp.float32)
    for c0 in range(0, n, chunk):
        sl = slice(c0, c0 + chunk)
        r = row_ref[0, :, sl]
        hit = lax.broadcasted_iota(jnp.int32, (rows, chunk), 0) == r
        zero = jnp.zeros((), jnp.float32)
        a = jnp.concatenate(
            [jnp.where(hit, hi_ref[0, :, sl], zero).astype(jnp.bfloat16),
             jnp.where(hit, lo_ref[0, :, sl], zero).astype(jnp.bfloat16)], axis=0)
        b = (lax.broadcasted_iota(jnp.int32, (width, chunk), 0) == col_ref[0, :, sl]).astype(jnp.bfloat16)
        total = total + lax.dot_general(a, b, (((1,), (1,)), ((), ())), preferred_element_type=jnp.float32)
    out_ref[...] += total[:rows] + total[rows:]


def deposit_all(values, cells, rows, width):
    sources, n = values.shape
    index = cells.astype(jnp.int32)
    row = (index // width)[:, None, :]
    col = (index % width)[:, None, :]
    hi = lax.reduce_precision(values, exponent_bits=8, mantissa_bits=7)
    lo = values - hi
    return pl.pallas_call(
        deposit_kernel,
        grid=(sources,),
        in_specs=[
            pl.BlockSpec((1, 1, n), lambda s: (s, 0, 0)),
            pl.BlockSpec((1, 1, n), lambda s: (s, 0, 0)),
            pl.BlockSpec((1, 1, n), lambda s: (s, 0, 0)),
            pl.BlockSpec((1, 1, n), lambda s: (s, 0, 0)),
        ],
        out_specs=pl.BlockSpec((rows, width), lambda s: (0, 0)),
        out_shape=jax.ShapeDtypeStruct((rows, width), jnp.float32),
    )(hi[:, None, :], lo[:, None, :], row, col)


def exchange(blocks, axis, count):
    me = lax.axis_index(axis)
    out = jnp.zeros_like(blocks)
    out = lax.dynamic_update_index_in_dim(out, lax.dynamic_index_in_dim(blocks, me, 0, keepdims=False), me, 0)
    for s in range(1, count):
        pairs = [(i, i ^ s) for i in range(count)]
        sent = lax.dynamic_index_in_dim(blocks, me ^ s, 0, keepdims=False)
        got = lax.ppermute(sent, axis, pairs)
        out = lax.dynamic_update_index_in_dim(out, got, me ^ s, 0)
    return out


def scatter_sum(x, axis, count):
    blocks = x.reshape((count, x.shape[0] // count) + x.shape[1:])
    return exchange(blocks, axis, count).sum(axis=0)


def gather_blocks(x, axis, count):
    me = lax.axis_index(axis)
    out = jnp.zeros((count,) + x.shape, x.dtype)
    out = lax.dynamic_update_index_in_dim(out, x, me, 0)
    for s in range(1, count):
        pairs = [(i, i ^ s) for i in range(count)]
        out = lax.dynamic_update_index_in_dim(out, lax.ppermute(x, axis, pairs), me ^ s, 0)
    return out.reshape((-1,) + x.shape[1:])


def sweep_kernel(pert_ref, a0_ref, a1_ref, halo_ref, cx_ref, cxh_ref, cy_ref, out_ref):
    kl = pert_ref.shape[0]
    nr, nq = a0_ref.shape
    span = nq + halo_ref.shape[2]
    coef = jnp.concatenate([cx_ref[0].T, cxh_ref[0]], axis=0)
    rows = lax.broadcasted_iota(jnp.int32, (nr, nq), 0)
    north = jnp.where(rows < nr - 1, cy_ref[0], 0.0)
    a0 = a0_ref[...]
    a1 = a1_ref[...]
    acc0 = jnp.zeros((nr, nq), jnp.float32)
    acc1 = jnp.zeros((nr, nq), jnp.float32)
    for k in range(kl):
        p0 = pert_ref[k, 0, 0].astype(jnp.float32)
        p1 = pert_ref[k, 1, 0].astype(jnp.float32)
        v = jnp.concatenate([(p0 * a0 + p1 * a1).T, halo_ref[k, 0]], axis=0)
        for step in range(SWEEPS):
            flux = coef * (pltpu.roll(v, span - 1, 0) - v)
            v = v + flux - pltpu.roll(flux, 1, 0)
        v = v[:nq].T
        for step in range(SWEEPS):
            flux = north * (pltpu.roll(v, nr - 1, 0) - v)
            v = v + flux - pltpu.roll(flux, 1, 0)
        acc0 = acc0 + p0 * v
        acc1 = acc1 + p1 * v
    out_ref[0, 0] = acc0
    out_ref[1, 0] = acc1


def turned(ring, halo):
    pad = -(-2 * halo // 8) * 8
    gap = jnp.zeros(ring.shape[:-1] + (pad - 2 * halo,), ring.dtype)
    block = jnp.concatenate([ring[..., :halo], gap, ring[..., -halo:]], axis=-1)
    return jnp.swapaxes(block, -1, -2)


def sweeps(perturb, field, halo, coef_x, coef_halo, coef_y):
    kl, nf, nl, nr, nq = perturb.shape
    assert nf == 2
    pad = halo.shape[2]
    return pl.pallas_call(
        sweep_kernel,
        grid=(nl,),
        in_specs=[
            pl.BlockSpec((kl, nf, 1, nr, nq), lambda l: (0, 0, l, 0, 0)),
            pl.BlockSpec((nr, nq), lambda l: (0, l)),
            pl.BlockSpec((nr, nq), lambda l: (0, nl + l)),
            pl.BlockSpec((kl, 1, pad, nr), lambda l: (0, l, 0, 0)),
            pl.BlockSpec((1, nr, nq), lambda l: (l, 0, 0)),
            pl.BlockSpec((1, pad, nr), lambda l: (l, 0, 0)),
            pl.BlockSpec((1, nr, nq), lambda l: (l, 0, 0)),
        ],
        out_specs=pl.BlockSpec((nf, 1, nr, nq), lambda l: (0, l, 0, 0)),
        out_shape=jax.ShapeDtypeStruct((nf, nl, nr, nq), jnp.float32),
    )(perturb, field, field, halo, coef_x, coef_halo, coef_y)


def on_device(perturb, coef_x, coef_y, obs_values, obs_tile, obs_cell):
    tiles = lax.axis_size("tile")
    mems = lax.axis_size("mem")
    kl, nf, nl, nr, nq = perturb.shape
    members = kl * mems
    halo = SWEEPS
    group = 32
    main = nf * nl * nq
    width = main + 128
    assert tiles >= 3 and tiles & (tiles - 1) == 0 and mems & (mems - 1) == 0
    assert nf * nl * group <= 128 and 2 * halo <= group
    forward = [(i, (i + 1) % tiles) for i in range(tiles)]
    backward = [((i + 1) % tiles, i) for i in range(tiles)]

    widened = perturb.astype(jnp.float32)
    flat = perturb.reshape((kl * nf * nl, nr, nq))
    lanes = jnp.arange(nq, dtype=jnp.int32)[:, None]
    picks = jnp.concatenate([jnp.arange(halo), jnp.arange(nq - halo, nq)]).astype(jnp.int32)[None, :]
    select = (lanes == picks).astype(jnp.bfloat16)
    rims = jnp.einsum("kyq,qe->kye", flat, select, preferred_element_type=jnp.float32)
    high = jnp.concatenate([rims[..., halo:], coef_x[..., -halo:]], axis=0)
    low = jnp.concatenate([rims[..., :halo], coef_x[..., :halo]], axis=0)
    from_left = lax.ppermute(high, "tile", forward)
    from_right = lax.ppermute(low, "tile", backward)

    target = obs_tile[:, 0]
    line = obs_cell // nq
    channel = line // nr
    row = line % nr
    column = obs_cell % nq
    dest = jnp.arange(tiles, dtype=jnp.int32)[:, None]
    apart = (target[None, :] - dest) % tiles
    home = channel * nq + column
    lower = main + channel * group + column
    upper = main + channel * group + group - nq + column
    place = jnp.where(apart == 0, home[None, :], jnp.where(apart == 1, lower[None, :], upper[None, :]))
    inside = (apart == 0) | ((apart == 1) & (column[None, :] < halo)) | (
        (apart == tiles - 1) & (column[None, :] >= nq - halo)
    )
    values = jnp.where(inside, obs_values[None, :], 0.0)
    cells = jnp.where(inside, row[None, :] * width + place, 0).astype(jnp.float32)
    outgoing = jnp.stack([values, cells], axis=1)
    me = lax.axis_index("tile")
    own = lax.dynamic_index_in_dim(outgoing, me, 0, keepdims=False)
    lists = [own]
    for s in range(1, tiles):
        pairs = [(i, i ^ s) for i in range(tiles)]
        sent = lax.dynamic_index_in_dim(outgoing, me ^ s, 0, keepdims=False)
        lists.append(lax.ppermute(sent, "tile", pairs))
    lists = jnp.stack(lists)
    field = deposit_all(lists[:, 0], lists[:, 1], nr, width)
    field = gather_blocks(scatter_sum(field, "mem", mems), "mem", mems)
    rim = jnp.transpose(field[:, main:].reshape(nr, nf, nl, group), (1, 2, 0, 3))

    count = kl * nf * nl
    left_p = from_left[:count].reshape((kl, nf, nl, nr, halo))
    right_p = from_right[:count].reshape((kl, nf, nl, nr, halo))
    left = jnp.sum(left_p * rim[None, ..., group - halo:], axis=1)
    right = jnp.sum(right_p * rim[None, ..., :halo], axis=1)
    pad = -(-2 * halo // 8) * 8
    gap = jnp.zeros(left.shape[:-1] + (pad - 2 * halo,), jnp.float32)
    ring = jnp.swapaxes(jnp.concatenate([right, gap, left], axis=-1), -1, -2)
    cgap = jnp.zeros((nl, nr, pad - 2 * halo), jnp.float32)
    cring = jnp.swapaxes(jnp.concatenate([from_right[count:], cgap, from_left[count:]], axis=-1), -1, -2)
    part = sweeps(perturb, field, ring, coef_x, cring, coef_y)
    blocks = part.reshape((nf, nl, mems, nr // mems, nq))
    blocks = jnp.transpose(blocks, (2, 0, 1, 3, 4))
    summed = jnp.transpose(exchange(blocks, "mem", mems).sum(axis=0), (2, 0, 1, 3))
    return summed / (members - 1)


def solution(mesh):
    return jax.shard_map(
        on_device,
        mesh=mesh,
        in_specs=(
            P("mem", None, None, None, "tile"),
            P(None, None, "tile"),
            P(None, None, "tile"),
            P(("mem", "tile")),
            P(("mem", "tile"), None),
            P(("mem", "tile")),
        ),
        out_specs=P("mem", None, None, "tile"),
        check_vma=False,
    )
```

```python
import jax
import jax.numpy as jnp
from jax import lax
from jax.experimental import pallas as pl
from jax.experimental.pallas import tpu as pltpu
from jax.sharding import PartitionSpec as P

FIELDS = 2
LEVELS = 2
SWEEPS = 6
LAT = 256


def sweep_north(field, coef):
    flux = coef[..., :-1, :] * (field[..., 1:, :] - field[..., :-1, :])
    zero_row = jnp.zeros(field.shape[:-2] + (1, field.shape[-1]), jnp.float32)
    upper = jnp.concatenate([flux, zero_row], axis=-2)
    lower = jnp.concatenate([zero_row, flux], axis=-2)
    return field + upper - lower


def deposit_kernel(hi_ref, lo_ref, row_ref, col_ref, out_ref):
    step = pl.program_id(0)

    @pl.when(step == 0)
    def _():
        out_ref[...] = jnp.zeros(out_ref.shape, jnp.float32)

    rows, width = out_ref.shape
    n = hi_ref.shape[2]
    chunk = 512
    total = jnp.zeros((2 * rows, width), jnp.float32)
    for c0 in range(0, n, chunk):
        sl = slice(c0, c0 + chunk)
        r = row_ref[0, :, sl]
        hit = lax.broadcasted_iota(jnp.int32, (rows, chunk), 0) == r
        zero = jnp.zeros((), jnp.float32)
        a = jnp.concatenate(
            [jnp.where(hit, hi_ref[0, :, sl], zero).astype(jnp.bfloat16),
             jnp.where(hit, lo_ref[0, :, sl], zero).astype(jnp.bfloat16)], axis=0)
        b = (lax.broadcasted_iota(jnp.int32, (width, chunk), 0) == col_ref[0, :, sl]).astype(jnp.bfloat16)
        total = total + lax.dot_general(a, b, (((1,), (1,)), ((), ())), preferred_element_type=jnp.float32)
    out_ref[...] += total[:rows] + total[rows:]


def deposit_all(values, cells, rows, width):
    sources, n = values.shape
    index = cells.astype(jnp.int32)
    row = (index // width)[:, None, :]
    col = (index % width)[:, None, :]
    hi = lax.reduce_precision(values, exponent_bits=8, mantissa_bits=7)
    lo = values - hi
    return pl.pallas_call(
        deposit_kernel,
        grid=(sources,),
        in_specs=[
            pl.BlockSpec((1, 1, n), lambda s: (s, 0, 0)),
            pl.BlockSpec((1, 1, n), lambda s: (s, 0, 0)),
            pl.BlockSpec((1, 1, n), lambda s: (s, 0, 0)),
            pl.BlockSpec((1, 1, n), lambda s: (s, 0, 0)),
        ],
        out_specs=pl.BlockSpec((rows, width), lambda s: (0, 0)),
        out_shape=jax.ShapeDtypeStruct((rows, width), jnp.float32),
    )(hi[:, None, :], lo[:, None, :], row, col)


def exchange(blocks, axis, count):
    me = lax.axis_index(axis)
    out = jnp.zeros_like(blocks)
    out = lax.dynamic_update_index_in_dim(out, lax.dynamic_index_in_dim(blocks, me, 0, keepdims=False), me, 0)
    for s in range(1, count):
        pairs = [(i, i ^ s) for i in range(count)]
        sent = lax.dynamic_index_in_dim(blocks, me ^ s, 0, keepdims=False)
        got = lax.ppermute(sent, axis, pairs)
        out = lax.dynamic_update_index_in_dim(out, got, me ^ s, 0)
    return out


def scatter_sum(x, axis, count):
    blocks = x.reshape((count, x.shape[0] // count) + x.shape[1:])
    return exchange(blocks, axis, count).sum(axis=0)


def gather_blocks(x, axis, count):
    me = lax.axis_index(axis)
    out = jnp.zeros((count,) + x.shape, x.dtype)
    out = lax.dynamic_update_index_in_dim(out, x, me, 0)
    for s in range(1, count):
        pairs = [(i, i ^ s) for i in range(count)]
        out = lax.dynamic_update_index_in_dim(out, lax.ppermute(x, axis, pairs), me ^ s, 0)
    return out.reshape((-1,) + x.shape[1:])


def sweep_kernel(pert_ref, a0_ref, a1_ref, halo_ref, cx_ref, cxh_ref, cy_ref, out_ref):
    kl = pert_ref.shape[0]
    nr, nq = a0_ref.shape
    span = nq + halo_ref.shape[2]
    coef = jnp.concatenate([cx_ref[0].T, cxh_ref[0]], axis=0)
    rows = lax.broadcasted_iota(jnp.int32, (nr, nq), 0)
    north = jnp.where(rows < nr - 1, cy_ref[0], 0.0)
    a0 = a0_ref[...]
    a1 = a1_ref[...]
    acc0 = jnp.zeros((nr, nq), jnp.float32)
    acc1 = jnp.zeros((nr, nq), jnp.float32)
    for k in range(kl):
        p0 = pert_ref[k, 0, 0].astype(jnp.float32)
        p1 = pert_ref[k, 1, 0].astype(jnp.float32)
        v = jnp.concatenate([(p0 * a0 + p1 * a1).T, halo_ref[k, 0]], axis=0)
        for step in range(SWEEPS):
            flux = coef * (pltpu.roll(v, span - 1, 0) - v)
            v = v + flux - pltpu.roll(flux, 1, 0)
        v = v[:nq].T
        for step in range(SWEEPS):
            flux = north * (pltpu.roll(v, nr - 1, 0) - v)
            v = v + flux - pltpu.roll(flux, 1, 0)
        acc0 = acc0 + p0 * v
        acc1 = acc1 + p1 * v
    out_ref[0, 0] = acc0
    out_ref[1, 0] = acc1


def turned(ring, halo):
    pad = -(-2 * halo // 8) * 8
    gap = jnp.zeros(ring.shape[:-1] + (pad - 2 * halo,), ring.dtype)
    block = jnp.concatenate([ring[..., :halo], gap, ring[..., -halo:]], axis=-1)
    return jnp.swapaxes(block, -1, -2)


def sweeps(perturb, field, halo, coef_x, coef_halo, coef_y):
    kl, nf, nl, nr, nq = perturb.shape
    assert nf == 2
    pad = halo.shape[2]
    return pl.pallas_call(
        sweep_kernel,
        grid=(nl,),
        in_specs=[
            pl.BlockSpec((kl, nf, 1, nr, nq), lambda l: (0, 0, l, 0, 0)),
            pl.BlockSpec((nr, nq), lambda l: (0, l)),
            pl.BlockSpec((nr, nq), lambda l: (0, nl + l)),
            pl.BlockSpec((kl, 1, pad, nr), lambda l: (0, l, 0, 0)),
            pl.BlockSpec((1, nr, nq), lambda l: (l, 0, 0)),
            pl.BlockSpec((1, pad, nr), lambda l: (l, 0, 0)),
            pl.BlockSpec((1, nr, nq), lambda l: (l, 0, 0)),
        ],
        out_specs=pl.BlockSpec((nf, 1, nr, nq), lambda l: (0, l, 0, 0)),
        out_shape=jax.ShapeDtypeStruct((nf, nl, nr, nq), jnp.float32),
    )(perturb, field, field, halo, coef_x, coef_halo, coef_y)


def on_device(perturb, coef_x, coef_y, obs_values, obs_tile, obs_cell):
    tiles = lax.axis_size("tile")
    mems = lax.axis_size("mem")
    kl, nf, nl, nr, nq = perturb.shape
    members = kl * mems
    halo = SWEEPS
    group = 32
    main = nf * nl * nq
    width = main + 128
    assert tiles >= 3 and tiles & (tiles - 1) == 0 and mems & (mems - 1) == 0
    assert nf * nl * group <= 128 and 2 * halo <= group
    forward = [(i, (i + 1) % tiles) for i in range(tiles)]
    backward = [((i + 1) % tiles, i) for i in range(tiles)]

    widened = perturb.astype(jnp.float32)
    flat = perturb.reshape((kl * nf * nl, nr, nq))
    high = jnp.concatenate([flat[..., -halo:].astype(jnp.float32), coef_x[..., -halo:]], axis=0)
    low = jnp.concatenate([flat[..., :halo].astype(jnp.float32), coef_x[..., :halo]], axis=0)
    from_left = lax.ppermute(high, "tile", forward)
    from_right = lax.ppermute(low, "tile", backward)

    target = obs_tile[:, 0]
    line = obs_cell // nq
    channel = line // nr
    row = line % nr
    column = obs_cell % nq
    dest = jnp.arange(tiles, dtype=jnp.int32)[:, None]
    apart = (target[None, :] - dest) % tiles
    home = channel * nq + column
    lower = main + channel * group + column
    upper = main + channel * group + group - nq + column
    place = jnp.where(apart == 0, home[None, :], jnp.where(apart == 1, lower[None, :], upper[None, :]))
    inside = (apart == 0) | ((apart == 1) & (column[None, :] < halo)) | (
        (apart == tiles - 1) & (column[None, :] >= nq - halo)
    )
    values = jnp.where(inside, obs_values[None, :], 0.0)
    cells = jnp.where(inside, row[None, :] * width + place, 0).astype(jnp.float32)
    outgoing = jnp.stack([values, cells], axis=1)
    me = lax.axis_index("tile")
    own = lax.dynamic_index_in_dim(outgoing, me, 0, keepdims=False)
    lists = []
    for s in range(1, tiles):
        pairs = [(i, i ^ s) for i in range(tiles)]
        sent = lax.dynamic_index_in_dim(outgoing, me ^ s, 0, keepdims=False)
        lists.append(lax.ppermute(sent, "tile", pairs))
    local = deposit_all(own[None, 0], own[None, 1], nr, width)
    lists = jnp.stack(lists)
    field = local + deposit_all(lists[:, 0], lists[:, 1], nr, width)
    field = gather_blocks(scatter_sum(field, "mem", mems), "mem", mems)
    rim = jnp.transpose(field[:, main:].reshape(nr, nf, nl, group), (1, 2, 0, 3))

    count = kl * nf * nl
    left_p = from_left[:count].reshape((kl, nf, nl, nr, halo))
    right_p = from_right[:count].reshape((kl, nf, nl, nr, halo))
    left = jnp.sum(left_p * rim[None, ..., group - halo:], axis=1)
    right = jnp.sum(right_p * rim[None, ..., :halo], axis=1)
    pad = -(-2 * halo // 8) * 8
    gap = jnp.zeros(left.shape[:-1] + (pad - 2 * halo,), jnp.float32)
    ring = jnp.swapaxes(jnp.concatenate([right, gap, left], axis=-1), -1, -2)
    cgap = jnp.zeros((nl, nr, pad - 2 * halo), jnp.float32)
    cring = jnp.swapaxes(jnp.concatenate([from_right[count:], cgap, from_left[count:]], axis=-1), -1, -2)
    part = sweeps(perturb, field, ring, coef_x, cring, coef_y)
    blocks = part.reshape((nf, nl, mems, nr // mems, nq))
    blocks = jnp.transpose(blocks, (2, 0, 1, 3, 4))
    summed = jnp.transpose(exchange(blocks, "mem", mems).sum(axis=0), (2, 0, 1, 3))
    return summed / (members - 1)


def solution(mesh):
    return jax.shard_map(
        on_device,
        mesh=mesh,
        in_specs=(
            P("mem", None, None, None, "tile"),
            P(None, None, "tile"),
            P(None, None, "tile"),
            P(("mem", "tile")),
            P(("mem", "tile"), None),
            P(("mem", "tile")),
        ),
        out_specs=P("mem", None, None, "tile"),
        check_vma=False,
    )
```
